128 devices in a mesh: req: 16 (over z, x), tp: 8 (over y, core).
Axes of the slice: x: 4, y: 4, z: 4, core: 2. Of those that a mesh axis runs over, the one named last changes fastest.
Arguments:
- queries: bfloat16 [512, 7168], P('req', 'tp')
- new_keys: bfloat16 [512, 1024], P('req', 'tp'), may hold values from -6 to 6
- new_values: bfloat16 [512, 1024], P('req', 'tp'), may hold values from -6 to 6
- cache_keys: bfloat16 [286720, 1024], P('req', 'tp'), may hold values from -6 to 6
- cache_values: bfloat16 [286720, 1024], P('req', 'tp'), may hold values from -6 to 6
- tok_req: int32 [512], P('req'), may hold values from 0 to 16, as said below
- cache_req: int32 [286720], P('req'), may hold values from -1 to 16, as said below
- out_weight: bfloat16 [7168, 7168], P('tp', 'req'), may hold values from -0.0625 to 0.0625
- residual: bfloat16 [512, 7168], P('tp', 'req')
- norm_gain: float32 [7168], replicated, may hold values from 0.1 to 1.9
- gate_weight: bfloat16 [7168, 20480], P(None, ('req', 'tp')), may hold values from -0.0625 to 0.0625
- up_weight: bfloat16 [7168, 20480], P(None, ('req', 'tp')), may hold values from -0.0625 to 0.0625
- down_weight: bfloat16 [20480, 7168], P(('req', 'tp')), may hold values from -0.15625 to 0.15625
Outputs:
- layer_out: bfloat16 [512, 7168], P('tp', 'req')
The draws below stay inside these ranges and needn't reach their ends.
Inputs may be any that keep to these rules, and one draw needn't show every extreme that they name: `tok_req`: within a group, request 0 is the prefill request, whose tokens stand first and in order; decode requests 1, 2, ... follow with one token each. `cache_req`: -1 marks an empty slot; within a group the owned slots stand first, each request's slots together, requests in increasing order; every request of a group that has tokens owns at least one slot.
All inputs are finite; a program needn't handle non-finite values.
Results may differ from the reference program's by a relative error of at most 0.014.
Values may be sent and summed in bfloat16 or wider, within the bound.
No kernel may reach another device: no remote copies, remote signals or barrier semaphores. Data moves between devices by JAX's collectives and lax.ppermute only.
A program may use at most 128 MiB of HBM per device.

```python
import math
import jax
import jax.numpy as jnp
from jax import lax

D = 7168
HEADS = 56
KVH = 8
HD = 128
FF = 20480
TG = 32
LONG = 8192
PREC = 1536
SHORT = 512
NGROUP = 16
TOK = 512
KB = 17920
POOL = 286720


def group_layout(key):
    key = jax.random.fold_in(key, 11)
    keys = jax.random.split(key, 6)
    prefill = (2 + jax.random.randint(keys[0], (NGROUP,), 0, 2).astype(jnp.int32)) * (TG // 4)
    half_group = jax.random.randint(keys[1], (), 0, NGROUP)
    prefill = jnp.where(jnp.arange(NGROUP) == half_group, 2 * (TG // 4), prefill).astype(jnp.int32)
    token_index = jnp.arange(TG, dtype=jnp.int32)
    tok_ids = jnp.where(token_index[None, :] < prefill[:, None], 0, token_index[None, :] - prefill[:, None] + 1).astype(jnp.int32)
    request_ids = jnp.arange(TG + 1, dtype=jnp.int32)
    decodes = TG - prefill
    long_flag = jax.random.randint(keys[2], (NGROUP,), 0, 2).astype(jnp.int32)
    prefill_len = jax.random.randint(keys[3], (NGROUP,), 1, PREC + 1).astype(jnp.int32)
    long_len = (LONG - jax.random.randint(keys[4], (NGROUP,), 0, LONG // 16)).astype(jnp.int32)
    short_len = jax.random.randint(keys[5], (NGROUP, TG + 1), 1, SHORT).astype(jnp.int32)
    decode_len = jnp.where((request_ids[None, :] == 1) & (long_flag[:, None] == 1), long_len[:, None], short_len)
    decode_len = jnp.where(request_ids[None, :] <= decodes[:, None], decode_len, 0)
    first_len = jnp.where(prefill > 0, prefill_len, 0)
    lengths = jnp.where(request_ids[None, :] == 0, first_len[:, None], decode_len).astype(jnp.int32)
    ends = jnp.cumsum(lengths, axis=1).astype(jnp.int32)
    slot_index = jnp.arange(KB, dtype=jnp.int32)
    owner = jnp.sum((slot_index[None, :, None] >= ends[:, None, :]).astype(jnp.int32), axis=2).astype(jnp.int32)
    owner = jnp.where(slot_index[None, :] < ends[:, -1:], owner, -1).astype(jnp.int32)
    return (tok_ids.reshape(TOK), owner.reshape(POOL))


def draw_tok_req(key, part):
    return group_layout(key)[0]


def draw_cache_req(key, part):
    return group_layout(key)[1]


def draw_queries(key, part):
    key = jax.random.fold_in(key, 23)
    first = jax.random.fold_in(key, 0)
    base = jax.random.normal(first, (TOK, HEADS, HD), jnp.float32)
    base = jnp.clip(base, -6.0, 6.0)
    return base.reshape(TOK, HEADS * HD).astype(jnp.bfloat16)


def draw_residual(key, part):
    key = jax.random.fold_in(key, 37)
    keys = jax.random.split(key, 3)
    column_rise = jnp.exp(math.log(3.0) * jnp.arange(D, dtype=jnp.float32) / (D - 1))
    column_scale = 0.4 * column_rise * jnp.exp(jax.random.uniform(keys[1], (D,), jnp.float32, 0.0, math.log(3.3)))
    row_scale = jnp.exp(jax.random.uniform(keys[2], (TOK, 1), jnp.float32, math.log(0.2), math.log(2.0)))
    base = jnp.clip(jax.random.normal(keys[0], (TOK, D), jnp.float32), -6.0, 6.0)
    return (base * row_scale * column_scale[None, :]).astype(jnp.bfloat16)


def with_spikes(values, key, source, target, shards_of, factor):
    def block_of(dim):
        return (jnp.arange(values.shape[dim]) // (values.shape[dim] // shards_of)).reshape((-1,) + (1,) * (values.ndim - 1 - dim))

    near = jax.random.permutation(key, shards_of)[block_of(target)]
    other_side = (block_of(target) + shards_of // 2) % shards_of
    return jnp.where((block_of(source) == near) | (block_of(source) == other_side), factor * values, values)


def block_levels(stream_key, dims, shards, low, high):
    gain = 1.0
    for axis_at, blocks in shards:
        draws = jax.random.uniform(jax.random.fold_in(jax.random.fold_in(stream_key, 6), axis_at), (blocks,), jnp.float32, low / len(shards), high / len(shards))
        gain = gain * jnp.repeat(jnp.exp(draws), dims[axis_at] // blocks).reshape((-1,) + (1,) * (len(dims) - 1 - axis_at))
    return gain


def gaussian(own_key, extent, scale, bound, pieces=(), kind=jnp.bfloat16):
    loudness = block_levels(own_key, extent, pieces, -0.22, 0.18) if pieces else 1.0
    values = jax.random.normal(own_key, extent, jnp.float32) * scale * loudness
    return jnp.minimum(jnp.maximum(values, -bound), bound).astype(kind)


def bell_draw_with(stream_key, dims, width, reach, cuts, heavy, kind=jnp.bfloat16):
    values = width * jax.random.normal(stream_key, dims, jnp.float32)
    if cuts:
        values = values * block_levels(stream_key, dims, cuts, -0.22, 0.18)
    return jnp.clip(with_spikes(values, jax.random.fold_in(stream_key, 3), *heavy), -reach, reach).astype(kind)


def setup_inputs(seed: int = 0) -> dict:
    key_list = jax.random.split(jax.random.key(seed), 14)
    queries = draw_queries(jax.random.fold_in(key_list[13], 71), 0)
    new_keys = gaussian(key_list[1], (TOK, KVH * HD), 1.0, 6.0, ((0, 16), (1, 8)))
    new_values = gaussian(key_list[2], (TOK, KVH * HD), 1.0, 6.0, ((0, 16), (1, 8)))
    cache_keys = gaussian(key_list[3], (POOL, KVH * HD), 1.0, 6.0, ((0, 16), (1, 8)))
    cache_values = gaussian(key_list[4], (POOL, KVH * HD), 1.0, 6.0, ((0, 16), (1, 8)))
    tok_req = draw_tok_req(jax.random.fold_in(key_list[13], 71), 0)
    cache_req = draw_cache_req(jax.random.fold_in(key_list[13], 71), 0)
    out_weight = gaussian(key_list[7], (HEADS * HD, D), (HEADS * HD) ** -0.5, 0.0625, ((0, 8), (1, 16)))
    residual = draw_residual(jax.random.fold_in(key_list[13], 71), 0)
    norm_gain = jnp.clip(1.0 + 0.18 * jax.random.normal(key_list[9], (D,), jnp.float32), 0.1, 1.9)
    gate_weight = gaussian(key_list[10], (D, FF), D ** -0.5, 0.0625, ((1, 128),))
    up_weight = gaussian(key_list[11], (D, FF), D ** -0.5, 0.0625, ((1, 128),))
    down_weight = bell_draw_with(key_list[12], (FF, D), FF ** -0.5, 0.15625, ((0, 128),), (0, 1, 128, 5.5))
    return {"queries": queries, "new_keys": new_keys, "new_values": new_values, "cache_keys": cache_keys, "cache_values": cache_values, "tok_req": tok_req, "cache_req": cache_req, "out_weight": out_weight, "residual": residual, "norm_gain": norm_gain, "gate_weight": gate_weight, "up_weight": up_weight, "down_weight": down_weight}


epsilon = 1e-05
masked_value = -1e+30

def group_attention(operands):
    group_queries, group_new_keys, group_new_values, group_cache_keys, group_cache_values, group_req, group_owner = operands
    group_size = HEADS // KVH
    keys_all = jnp.concatenate([group_cache_keys, group_new_keys], axis=0).astype(jnp.float32).reshape(KB + TG, KVH, HD)
    values_all = jnp.concatenate([group_cache_values, group_new_values], axis=0).astype(jnp.float32).reshape(KB + TG, KVH, HD)
    query_all = group_queries.astype(jnp.float32).reshape(TG, KVH, group_size, HD)
    scores = jnp.einsum('ikgd,jkd->kgij', query_all, keys_all) / math.sqrt(HD)
    cache_seen = group_owner[None, :] == group_req[:, None]
    positions = jnp.arange(TG, dtype=jnp.int32)
    new_seen = (group_req[None, :] == group_req[:, None]) & (positions[None, :] <= positions[:, None])
    visible = jnp.concatenate([cache_seen, new_seen], axis=1)
    masked = jnp.where(visible[None, None], scores, masked_value)
    row_max = lax.optimization_barrier(jnp.max(masked, axis=-1, keepdims=True))
    probs = jnp.where(visible[None, None], jnp.exp(masked - row_max), 0.0)
    probs = lax.optimization_barrier(probs.astype(jnp.bfloat16)).astype(jnp.float32)
    denominator = lax.optimization_barrier(jnp.sum(probs, axis=-1))
    weighted = jnp.einsum('kgij,jkd->ikgd', probs, values_all)
    result = weighted / jnp.transpose(denominator, (2, 0, 1))[..., None]
    return result.astype(jnp.bfloat16).reshape(TG, HEADS * HD)

def reference(queries, new_keys, new_values, cache_keys, cache_values, tok_req, cache_req, out_weight, residual, norm_gain, gate_weight, up_weight, down_weight):
    operands = (queries.reshape(NGROUP, TG, HEADS * HD), new_keys.reshape(NGROUP, TG, KVH * HD), new_values.reshape(NGROUP, TG, KVH * HD), cache_keys.reshape(NGROUP, KB, KVH * HD), cache_values.reshape(NGROUP, KB, KVH * HD), tok_req.reshape(NGROUP, TG), cache_req.reshape(NGROUP, KB))
    attended = lax.map(group_attention, operands).reshape(TOK, HEADS * HD)
    projected = jnp.dot(attended, out_weight, preferred_element_type=jnp.float32)
    stream = (residual.astype(jnp.float32) + projected).astype(jnp.bfloat16)
    wide = stream.astype(jnp.float32)
    mean_square = lax.optimization_barrier(jnp.mean(wide * wide, axis=1, keepdims=True))
    normed = (wide * lax.rsqrt(mean_square + epsilon) * norm_gain.astype(jnp.float32)[None, :]).astype(jnp.bfloat16)
    gate = jnp.dot(normed, gate_weight, preferred_element_type=jnp.float32)
    up = jnp.dot(normed, up_weight, preferred_element_type=jnp.float32)
    hidden = (jax.nn.silu(gate) * up).astype(jnp.bfloat16)
    mlp = jnp.dot(hidden, down_weight, preferred_element_type=jnp.float32)
    return (wide + mlp).astype(jnp.bfloat16)
```

```python
import math

import jax
import jax.numpy as jnp
from jax import lax
from jax.sharding import PartitionSpec as P

HD = 128


epsilon = 1e-05
masked_value = -1e30
key_block = 2560


def attend(queries, new_keys, new_values, cache_keys, cache_values, tok_req, cache_req):
    tokens_here = queries.shape[0]
    head_dim = HD
    kv_here = new_keys.shape[1] // head_dim
    group_size = queries.shape[1] // (kv_here * head_dim)
    score_scale = 1.0 / math.sqrt(head_dim)
    row_count = tokens_here * group_size
    grouped = queries.reshape(tokens_here, kv_here, group_size, head_dim)
    row_req = jnp.repeat(tok_req, group_size)
    row_tok = jnp.repeat(jnp.arange(tokens_here, dtype=jnp.int32), group_size)
    pool_size = cache_keys.shape[0]
    block_width = min(key_block, pool_size)
    live_slots = jnp.sum((cache_req >= 0).astype(jnp.int32))
    live_blocks = (live_slots + block_width - 1) // block_width

    def update(carried, block_keys, block_values, visible):
        running_max, denominator, weighted = carried[0]
        query_rows = grouped[:, 0].reshape(row_count, head_dim)
        scores = (
            jnp.einsum("qd,kd->qk", query_rows, block_keys, preferred_element_type=jnp.float32)
            * score_scale
        )
        masked = jnp.where(visible, scores, masked_value)
        new_max = jnp.maximum(running_max, jnp.max(masked, axis=1))
        weights = jnp.where(visible, jnp.exp(masked - new_max[:, None]), 0.0).astype(jnp.bfloat16)
        factor = jnp.exp(running_max - new_max)
        denominator = denominator * factor + jnp.sum(weights.astype(jnp.float32), axis=1)
        weighted = weighted * factor[:, None] + jnp.dot(
            weights, block_values, preferred_element_type=jnp.float32
        )
        renewed = [(new_max, denominator, weighted)]
        return tuple(renewed)

    initial = tuple(
        (
            (
                jnp.full((row_count,), masked_value, jnp.float32),
                jnp.zeros((row_count,), jnp.float32),
                jnp.zeros((row_count, head_dim), jnp.float32),
            )
            for unused in range(kv_here)
        )
    )

    def consume(block_index, carried):
        first_slot = block_index * block_width
        block_keys = lax.dynamic_slice_in_dim(cache_keys, first_slot, block_width, 0)
        block_values = lax.dynamic_slice_in_dim(cache_values, first_slot, block_width, 0)
        owners = lax.dynamic_slice_in_dim(cache_req, first_slot, block_width, 0)
        visible = owners[None, :] == row_req[:, None]
        return update(carried, block_keys, block_values, visible)

    carried = lax.fori_loop(0, live_blocks, consume, initial)
    causal = (tok_req[None, :] == row_req[:, None]) & (
        jnp.arange(tokens_here, dtype=jnp.int32)[None, :] <= row_tok[:, None]
    )
    carried = update(carried, new_keys, new_values, causal)
    per_head = [
        (weighted / denominator[:, None]).reshape(tokens_here, group_size, head_dim)
        for running_max, denominator, weighted in carried
    ]
    return (
        jnp.stack(per_head, axis=1)
        .reshape(tokens_here, kv_here * group_size * head_dim)
        .astype(jnp.bfloat16)
    )


def per_device(
    queries,
    new_keys,
    new_values,
    cache_keys,
    cache_values,
    tok_req,
    cache_req,
    out_weight,
    residual,
    norm_gain,
    gate_weight,
    up_weight,
    down_weight,
):
    attended = attend(queries, new_keys, new_values, cache_keys, cache_values, tok_req, cache_req)
    partial_out = jnp.dot(
        lax.all_gather(attended, "req", axis=0, tiled=True),
        out_weight,
        preferred_element_type=jnp.float32,
    )
    mixed = lax.psum_scatter(
        partial_out.astype(jnp.bfloat16), "tp", scatter_dimension=0, tiled=True
    ).astype(jnp.float32)
    stream = (residual.astype(jnp.float32) + mixed).astype(jnp.bfloat16)
    req_count = lax.axis_size("req")
    tp_count = lax.axis_size("tp")
    full_stream = lax.all_gather(
        lax.all_gather(stream, "req", axis=1, tiled=True), "tp", axis=0, tiled=True
    )
    wide_full = full_stream.astype(jnp.float32)
    mean_square = jnp.mean(wide_full * wide_full, axis=1, keepdims=True)
    normed = (wide_full * lax.rsqrt(mean_square + epsilon) * norm_gain[None, :]).astype(
        jnp.bfloat16
    )
    gate = jnp.dot(normed, gate_weight, preferred_element_type=jnp.float32)
    up = jnp.dot(normed, up_weight, preferred_element_type=jnp.float32)
    hidden = (jax.nn.silu(gate) * up).astype(jnp.bfloat16)
    total_tokens, hidden_here = hidden.shape
    tokens_out = total_tokens // tp_count
    columns = down_weight.shape[1] // req_count
    product = jnp.einsum(
        "tsh,hrf->rtsf",
        hidden.reshape(tp_count, tokens_out, hidden_here),
        down_weight.reshape(hidden_here, req_count, columns),
        preferred_element_type=jnp.float32,
    )
    pieces = product.astype(jnp.bfloat16).reshape(req_count * tp_count, tokens_out, columns)
    received = lax.all_to_all(pieces, ("req", "tp"), 0, 0, tiled=True)
    summed = jnp.sum(received.astype(jnp.float32), axis=0)
    return (stream.astype(jnp.float32) + summed).astype(jnp.bfloat16)


def solution(mesh):
    in_specs = (
        P("req", "tp"),
        P("req", "tp"),
        P("req", "tp"),
        P("req", "tp"),
        P("req", "tp"),
        P("req"),
        P("req"),
        P("tp", "req"),
        P("tp", "req"),
        P(),
        P(None, ("req", "tp")),
        P(None, ("req", "tp")),
        P(("req", "tp"), None),
    )
    out_specs = P("tp", "req")
    return jax.shard_map(
        per_device, mesh=mesh, in_specs=in_specs, out_specs=out_specs, check_vma=False
    )
```

```python
import math

import jax
import jax.numpy as jnp
from jax import lax
from jax.sharding import PartitionSpec as P

HD = 128


epsilon = 1e-05
masked_value = -1e30
key_block = 2560


def attend(queries, new_keys, new_values, cache_keys, cache_values, tok_req, cache_req):
    tokens_here = queries.shape[0]
    head_dim = HD
    kv_here = new_keys.shape[1] // head_dim
    group_size = queries.shape[1] // (kv_here * head_dim)
    score_scale = 1.0 / math.sqrt(head_dim)
    row_count = tokens_here * group_size
    grouped = queries.reshape(tokens_here, kv_here, group_size, head_dim)
    row_req = jnp.repeat(tok_req, group_size)
    row_tok = jnp.repeat(jnp.arange(tokens_here, dtype=jnp.int32), group_size)
    pool_size = cache_keys.shape[0]
    block_width = min(key_block, pool_size)
    live_slots = jnp.sum((cache_req >= 0).astype(jnp.int32))
    live_blocks = (live_slots + block_width - 1) // block_width

    def update(carried, block_keys, block_values, visible):
        running_max, denominator, weighted = carried[0]
        query_rows = grouped[:, 0].reshape(row_count, head_dim)
        scores = (
            jnp.einsum("qd,kd->qk", query_rows, block_keys, preferred_element_type=jnp.float32)
            * score_scale
        )
        masked = jnp.where(visible, scores, masked_value)
        new_max = jnp.maximum(running_max, jnp.max(masked, axis=1))
        weights = jnp.where(visible, jnp.exp(masked - new_max[:, None]), 0.0).astype(jnp.bfloat16)
        factor = jnp.exp(running_max - new_max)
        denominator = denominator * factor + jnp.sum(weights.astype(jnp.float32), axis=1)
        weighted = weighted * factor[:, None] + jnp.dot(
            weights, block_values, preferred_element_type=jnp.float32
        )
        renewed = [(new_max, denominator, weighted)]
        return tuple(renewed)

    initial = tuple(
        (
            (
                jnp.full((row_count,), masked_value, jnp.float32),
                jnp.zeros((row_count,), jnp.float32),
                jnp.zeros((row_count, head_dim), jnp.float32),
            )
            for unused in range(kv_here)
        )
    )

    def consume(block_index, carried):
        first_slot = block_index * block_width
        block_keys = lax.dynamic_slice_in_dim(cache_keys, first_slot, block_width, 0)
        block_values = lax.dynamic_slice_in_dim(cache_values, first_slot, block_width, 0)
        owners = lax.dynamic_slice_in_dim(cache_req, first_slot, block_width, 0)
        visible = owners[None, :] == row_req[:, None]
        return update(carried, block_keys, block_values, visible)

    carried = lax.fori_loop(0, live_blocks, consume, initial)
    causal = (tok_req[None, :] == row_req[:, None]) & (
        jnp.arange(tokens_here, dtype=jnp.int32)[None, :] <= row_tok[:, None]
    )
    carried = update(carried, new_keys, new_values, causal)
    per_head = [
        (weighted / denominator[:, None]).reshape(tokens_here, group_size, head_dim)
        for running_max, denominator, weighted in carried
    ]
    return (
        jnp.stack(per_head, axis=1)
        .reshape(tokens_here, kv_here * group_size * head_dim)
        .astype(jnp.bfloat16)
    )


def per_device(
    queries,
    new_keys,
    new_values,
    cache_keys,
    cache_values,
    tok_req,
    cache_req,
    out_weight,
    residual,
    norm_gain,
    gate_weight,
    up_weight,
    down_weight,
):
    swap = [(0, 1), (1, 0)]
    gate_partner = lax.ppermute(gate_weight, "core", swap)
    up_partner = lax.ppermute(up_weight, "core", swap)
    down_partner = lax.ppermute(down_weight, "core", swap)
    attended = attend(queries, new_keys, new_values, cache_keys, cache_values, tok_req, cache_req)
    partial_out = jnp.dot(
        lax.all_gather(attended, "req", axis=0, tiled=True),
        out_weight,
        preferred_element_type=jnp.float32,
    )
    mixed = lax.psum_scatter(
        partial_out.astype(jnp.bfloat16), ("y", "core"), scatter_dimension=0, tiled=True
    ).astype(jnp.float32)
    stream = (residual.astype(jnp.float32) + mixed).astype(jnp.bfloat16)
    req_count = lax.axis_size("req")
    y_count = lax.axis_size("y")
    tokens_out, columns = stream.shape
    gathered = lax.all_gather(stream, ("req", "y"), axis=0, tiled=True)
    side_stream = (
        gathered.reshape(req_count, y_count, tokens_out, columns)
        .transpose(1, 2, 0, 3)
        .reshape(y_count * tokens_out, req_count * columns)
    )
    wide_side = side_stream.astype(jnp.float32)
    mean_square = jnp.mean(wide_side * wide_side, axis=1, keepdims=True)
    normed = (wide_side * lax.rsqrt(mean_square + epsilon) * norm_gain[None, :]).astype(
        jnp.bfloat16
    )

    def hidden_of(gate_w, up_w):
        gate = jnp.dot(normed, gate_w, preferred_element_type=jnp.float32)
        up = jnp.dot(normed, up_w, preferred_element_type=jnp.float32)
        hidden = (jax.nn.silu(gate) * up).astype(jnp.bfloat16)
        return hidden.reshape(y_count, tokens_out, hidden.shape[1])

    def down_of(hidden, down_w):
        return jnp.einsum(
            "ysh,hrf->rysf",
            hidden,
            down_w.reshape(down_w.shape[0], req_count, columns),
            preferred_element_type=jnp.float32,
        )

    product = down_of(hidden_of(gate_weight, up_weight), down_weight) + down_of(
        hidden_of(gate_partner, up_partner), down_partner
    )
    pieces = product.astype(jnp.bfloat16).reshape(req_count * y_count, tokens_out, columns)
    received = lax.all_to_all(pieces, ("req", "y"), 0, 0, tiled=True)
    summed = jnp.sum(received.astype(jnp.float32), axis=0)
    return (stream.astype(jnp.float32) + summed).astype(jnp.bfloat16)


def solution(mesh):
    req_count, tp_count = mesh.devices.shape
    split = jax.sharding.Mesh(
        mesh.devices.reshape(req_count, tp_count // 2, 2), ("req", "y", "core")
    )
    tp = ("y", "core")
    in_specs = (
        P("req", tp),
        P("req", tp),
        P("req", tp),
        P("req", tp),
        P("req", tp),
        P("req"),
        P("req"),
        P(tp, "req"),
        P(tp, "req"),
        P(),
        P(None, ("req",) + tp),
        P(None, ("req",) + tp),
        P(("req",) + tp, None),
    )
    out_specs = P(tp, "req")
    return jax.shard_map(
        per_device, mesh=split, in_specs=in_specs, out_specs=out_specs, check_vma=False
    )
```

```python
import math

import jax
import jax.numpy as jnp
from jax import lax
from jax.sharding import PartitionSpec as P

HD = 128


epsilon = 1e-05
masked_value = -1e30
key_block = 2560


def attend(queries, new_keys, new_values, cache_keys, cache_values, tok_req, cache_req):
    tokens_here = queries.shape[0]
    head_dim = HD
    kv_here = new_keys.shape[1] // head_dim
    group_size = queries.shape[1] // (kv_here * head_dim)
    score_scale = 1.0 / math.sqrt(head_dim)
    row_count = tokens_here * group_size
    grouped = queries.reshape(tokens_here, kv_here, group_size, head_dim)
    row_req = jnp.repeat(tok_req, group_size)
    row_tok = jnp.repeat(jnp.arange(tokens_here, dtype=jnp.int32), group_size)
    pool_size = cache_keys.shape[0]
    block_width = min(key_block, pool_size)
    live_slots = jnp.sum((cache_req >= 0).astype(jnp.int32))
    live_blocks = (live_slots + block_width - 1) // block_width

    def update(carried, block_keys, block_values, visible):
        running_max, denominator, weighted = carried[0]
        query_rows = grouped[:, 0].reshape(row_count, head_dim)
        scores = (
            jnp.einsum("qd,kd->qk", query_rows, block_keys, preferred_element_type=jnp.float32)
            * score_scale
        )
        masked = jnp.where(visible, scores, masked_value)
        new_max = jnp.maximum(running_max, jnp.max(masked, axis=1))
        weights = jnp.where(visible, jnp.exp(masked - new_max[:, None]), 0.0).astype(jnp.bfloat16)
        factor = jnp.exp(running_max - new_max)
        denominator = denominator * factor + jnp.sum(weights.astype(jnp.float32), axis=1)
        weighted = weighted * factor[:, None] + jnp.dot(
            weights, block_values, preferred_element_type=jnp.float32
        )
        renewed = [(new_max, denominator, weighted)]
        return tuple(renewed)

    initial = tuple(
        (
            (
                jnp.full((row_count,), masked_value, jnp.float32),
                jnp.zeros((row_count,), jnp.float32),
                jnp.zeros((row_count, head_dim), jnp.float32),
            )
            for unused in range(kv_here)
        )
    )

    def consume(block_index, carried):
        first_slot = block_index * block_width
        block_keys = lax.dynamic_slice_in_dim(cache_keys, first_slot, block_width, 0)
        block_values = lax.dynamic_slice_in_dim(cache_values, first_slot, block_width, 0)
        owners = lax.dynamic_slice_in_dim(cache_req, first_slot, block_width, 0)
        visible = owners[None, :] == row_req[:, None]
        return update(carried, block_keys, block_values, visible)

    carried = lax.fori_loop(0, live_blocks, consume, initial)
    causal = (tok_req[None, :] == row_req[:, None]) & (
        jnp.arange(tokens_here, dtype=jnp.int32)[None, :] <= row_tok[:, None]
    )
    carried = update(carried, new_keys, new_values, causal)
    per_head = [
        (weighted / denominator[:, None]).reshape(tokens_here, group_size, head_dim)
        for running_max, denominator, weighted in carried
    ]
    return (
        jnp.stack(per_head, axis=1)
        .reshape(tokens_here, kv_here * group_size * head_dim)
        .astype(jnp.bfloat16)
    )


def per_device(
    queries,
    new_keys,
    new_values,
    cache_keys,
    cache_values,
    tok_req,
    cache_req,
    out_weight,
    residual,
    norm_gain,
    gate_weight,
    up_weight,
    down_weight,
):
    swap = [(0, 1), (1, 0)]
    gate_partner = lax.ppermute(gate_weight, "core", swap)
    up_partner = lax.ppermute(up_weight, "core", swap)
    down_partner = lax.ppermute(down_weight, "core", swap)
    attended = attend(queries, new_keys, new_values, cache_keys, cache_values, tok_req, cache_req)
    partial_out = jnp.dot(
        lax.all_gather(attended, "req", axis=0, tiled=True),
        out_weight,
        preferred_element_type=jnp.float32,
    )
    mixed = lax.psum_scatter(
        partial_out.astype(jnp.bfloat16), ("y", "core"), scatter_dimension=0, tiled=True
    ).astype(jnp.float32)
    stream = (residual.astype(jnp.float32) + mixed).astype(jnp.bfloat16)
    req_count = lax.axis_size("req")
    y_count = lax.axis_size("y")
    tokens_out, columns = stream.shape
    side_stream = lax.all_gather(
        lax.all_gather(stream, "req", axis=1, tiled=True), "y", axis=0, tiled=True
    )
    wide_side = side_stream.astype(jnp.float32)
    mean_square = jnp.mean(wide_side * wide_side, axis=1, keepdims=True)
    normed = (wide_side * lax.rsqrt(mean_square + epsilon) * norm_gain[None, :]).astype(
        jnp.bfloat16
    )

    def hidden_of(gate_w, up_w):
        gate = jnp.dot(normed, gate_w, preferred_element_type=jnp.float32)
        up = jnp.dot(normed, up_w, preferred_element_type=jnp.float32)
        hidden = (jax.nn.silu(gate) * up).astype(jnp.bfloat16)
        return hidden.reshape(y_count, tokens_out, hidden.shape[1])

    def down_of(hidden, down_w):
        return jnp.einsum(
            "ysh,hrf->rysf",
            hidden,
            down_w.reshape(down_w.shape[0], req_count, columns),
            preferred_element_type=jnp.float32,
        )

    product = down_of(hidden_of(gate_weight, up_weight), down_weight) + down_of(
        hidden_of(gate_partner, up_partner), down_partner
    )
    pieces = product.astype(jnp.bfloat16).reshape(req_count * y_count, tokens_out, columns)
    received = lax.all_to_all(pieces, ("req", "y"), 0, 0, tiled=True)
    summed = jnp.sum(received.astype(jnp.float32), axis=0)
    return (stream.astype(jnp.float32) + summed).astype(jnp.bfloat16)


def solution(mesh):
    req_count, tp_count = mesh.devices.shape
    split = jax.sharding.Mesh(
        mesh.devices.reshape(req_count, tp_count // 2, 2), ("req", "y", "core")
    )
    tp = ("y", "core")
    in_specs = (
        P("req", tp),
        P("req", tp),
        P("req", tp),
        P("req", tp),
        P("req", tp),
        P("req"),
        P("req"),
        P(tp, "req"),
        P(tp, "req"),
        P(),
        P(None, ("req",) + tp),
        P(None, ("req",) + tp),
        P(("req",) + tp, None),
    )
    out_specs = P(tp, "req")
    return jax.shard_map(
        per_device, mesh=split, in_specs=in_specs, out_specs=out_specs, check_vma=False
    )
```

```python
import math

import jax
import jax.numpy as jnp
from jax import lax
from jax.sharding import PartitionSpec as P


HD = 128


epsilon = 1e-05
masked_value = -1e30
key_block = 2560


def attend(queries, new_keys, new_values, cache_keys, cache_values, tok_req, cache_req):
    tokens_here = queries.shape[0]
    head_dim = HD
    kv_here = new_keys.shape[1] // head_dim
    group_size = queries.shape[1] // (kv_here * head_dim)
    score_scale = 1.0 / math.sqrt(head_dim)
    row_count = tokens_here * group_size
    grouped = queries.reshape(tokens_here, kv_here, group_size, head_dim)
    row_req = jnp.repeat(tok_req, group_size)
    row_tok = jnp.repeat(jnp.arange(tokens_here, dtype=jnp.int32), group_size)
    pool_size = cache_keys.shape[0]
    block_width = min(key_block, pool_size)
    live_slots = jnp.sum((cache_req >= 0).astype(jnp.int32))
    live_blocks = (live_slots + block_width - 1) // block_width

    def update(carried, block_keys, block_values, visible):
        running_max, denominator, weighted = carried[0]
        query_rows = grouped[:, 0].reshape(row_count, head_dim)
        scores = (
            jnp.einsum("qd,kd->qk", query_rows, block_keys, preferred_element_type=jnp.float32)
            * score_scale
        )
        masked = jnp.where(visible, scores, masked_value)
        new_max = jnp.maximum(running_max, jnp.max(masked, axis=1))
        weights = jnp.where(visible, jnp.exp(masked - new_max[:, None]), 0.0).astype(jnp.bfloat16)
        factor = jnp.exp(running_max - new_max)
        denominator = denominator * factor + jnp.sum(weights.astype(jnp.float32), axis=1)
        weighted = weighted * factor[:, None] + jnp.dot(
            weights, block_values, preferred_element_type=jnp.float32
        )
        renewed = [(new_max, denominator, weighted)]
        return tuple(renewed)

    initial = tuple(
        (
            (
                jnp.full((row_count,), masked_value, jnp.float32),
                jnp.zeros((row_count,), jnp.float32),
                jnp.zeros((row_count, head_dim), jnp.float32),
            )
            for _ in range(kv_here)
        )
    )

    def consume(block_index, carried):
        first_slot = block_index * block_width
        block_keys = lax.dynamic_slice_in_dim(cache_keys, first_slot, block_width, 0)
        block_values = lax.dynamic_slice_in_dim(cache_values, first_slot, block_width, 0)
        owners = lax.dynamic_slice_in_dim(cache_req, first_slot, block_width, 0)
        visible = owners[None, :] == row_req[:, None]
        return update(carried, block_keys, block_values, visible)

    carried = lax.fori_loop(0, live_blocks, consume, initial)
    causal = (tok_req[None, :] == row_req[:, None]) & (
        jnp.arange(tokens_here, dtype=jnp.int32)[None, :] <= row_tok[:, None]
    )
    carried = update(carried, new_keys, new_values, causal)
    per_head = [
        (weighted / denominator[:, None]).reshape(tokens_here, group_size, head_dim)
        for running_max, denominator, weighted in carried
    ]
    return (
        jnp.stack(per_head, axis=1)
        .reshape(tokens_here, kv_here * group_size * head_dim)
        .astype(jnp.bfloat16)
    )


def per_device(
    queries,
    new_keys,
    new_values,
    cache_keys,
    cache_values,
    tok_req,
    cache_req,
    out_weight,
    residual,
    norm_gain,
    gate_weight,
    up_weight,
    down_weight,
):
    swap = [(0, 1), (1, 0)]
    req_count = lax.axis_size("req")
    columns = down_weight.shape[1] // req_count
    down_blocks = down_weight.reshape(down_weight.shape[0], req_count, columns)
    gate_partner = lax.ppermute(gate_weight, "core", swap)
    up_partner = lax.ppermute(up_weight, "core", swap)
    down_partner = lax.ppermute(down_blocks, "core", swap)
    attended = attend(queries, new_keys, new_values, cache_keys, cache_values, tok_req, cache_req)
    partial_out = jnp.dot(
        lax.all_gather(attended, "req", axis=0, tiled=True),
        out_weight,
        preferred_element_type=jnp.float32,
    )
    mixed = lax.psum_scatter(
        partial_out.astype(jnp.bfloat16), ("y", "core"), scatter_dimension=0, tiled=True
    ).astype(jnp.float32)
    stream = (residual.astype(jnp.float32) + mixed).astype(jnp.bfloat16)
    y_count = lax.axis_size("y")
    tokens_out = stream.shape[0]
    side_stream = lax.all_gather(
        lax.all_gather(stream, "req", axis=1, tiled=True), "y", axis=0, tiled=True
    )
    wide_side = side_stream.astype(jnp.float32)
    mean_square = jnp.mean(wide_side * wide_side, axis=1, keepdims=True)
    normed = (wide_side * lax.rsqrt(mean_square + epsilon) * norm_gain[None, :]).astype(
        jnp.bfloat16
    )

    def hidden_of(gate_w, up_w):
        gate = jnp.dot(normed, gate_w, preferred_element_type=jnp.float32)
        up = jnp.dot(normed, up_w, preferred_element_type=jnp.float32)
        hidden = (jax.nn.silu(gate) * up).astype(jnp.bfloat16)
        return hidden.reshape(y_count, tokens_out, hidden.shape[1])

    def down_of(hidden, down_w):
        return jnp.einsum(
            "ysh,hrf->rysf",
            hidden,
            down_w,
            preferred_element_type=jnp.float32,
        )

    product = down_of(hidden_of(gate_weight, up_weight), down_blocks) + down_of(
        hidden_of(gate_partner, up_partner), down_partner
    )
    pieces = product.astype(jnp.bfloat16).reshape(req_count * y_count, tokens_out, columns)
    received = lax.all_to_all(pieces, ("req", "y"), 0, 0, tiled=True)
    summed = jnp.sum(received.astype(jnp.float32), axis=0)
    return (stream.astype(jnp.float32) + summed).astype(jnp.bfloat16)


def solution(mesh):
    req_count, tp_count = mesh.devices.shape
    split = jax.sharding.Mesh(
        mesh.devices.reshape(req_count, tp_count // 2, 2), ("req", "y", "core")
    )
    tp = ("y", "core")
    in_specs = (
        P("req", tp),
        P("req", tp),
        P("req", tp),
        P("req", tp),
        P("req", tp),
        P("req"),
        P("req"),
        P(tp, "req"),
        P(tp, "req"),
        P(),
        P(None, ("req",) + tp),
        P(None, ("req",) + tp),
        P(("req",) + tp, None),
    )
    out_specs = P(tp, "req")
    return jax.shard_map(
        per_device, mesh=split, in_specs=in_specs, out_specs=out_specs, check_vma=False
    )
```

```python
import functools
import math

import jax
import jax.numpy as jnp
from jax import lax
from jax.experimental import pallas as pl
from jax.experimental.pallas import tpu as pltpu
from jax.sharding import PartitionSpec as P


HD = 128


epsilon = 1e-05
masked_value = -1e30
key_block = 1792


def _cache_kernel(live_ref, q_ref, k_ref, v_ref, owner_ref, rowreq_ref, m_out, l_out, acc_out, m_s, l_s, acc_s, *, scale):
    i = pl.program_id(0)

    @pl.when(i == 0)
    def _init():
        m_s[...] = jnp.full(m_s.shape, masked_value, jnp.float32)
        l_s[...] = jnp.zeros(l_s.shape, jnp.float32)
        acc_s[...] = jnp.zeros(acc_s.shape, jnp.float32)

    @pl.when(i < live_ref[0])
    def _step():
        scores = lax.dot_general(q_ref[...], k_ref[...], (((1,), (1,)), ((), ())),
                                 preferred_element_type=jnp.float32) * scale
        visible = owner_ref[...] == rowreq_ref[...]
        masked = jnp.where(visible, scores, masked_value)
        running = m_s[...]
        new_max = jnp.maximum(running, jnp.max(masked, axis=1, keepdims=True))
        weights = jnp.where(visible, jnp.exp(masked - new_max), 0.0).astype(jnp.bfloat16)
        factor = jnp.exp(running - new_max)
        l_s[...] = l_s[...] * factor + jnp.sum(weights.astype(jnp.float32), axis=1, keepdims=True)
        acc_s[...] = acc_s[...] * factor + jnp.dot(weights, v_ref[...], preferred_element_type=jnp.float32)
        m_s[...] = new_max

    @pl.when(i == pl.num_programs(0) - 1)
    def _done():
        m_out[...] = m_s[...]
        l_out[...] = l_s[...]
        acc_out[...] = acc_s[...]


def cache_attention(query_rows, cache_keys, cache_values, cache_req, row_req, live_blocks, block, scale):
    rows, hd = query_rows.shape
    pool = cache_keys.shape[0]
    nb = pool // block

    def kv_map(i, live):
        return (jnp.maximum(jnp.minimum(i, live[0] - 1), 0), 0)

    def own_map(i, live):
        return (0, jnp.maximum(jnp.minimum(i, live[0] - 1), 0))

    full = lambda i, live: (0, 0)
    grid_spec = pltpu.PrefetchScalarGridSpec(
        num_scalar_prefetch=1,
        grid=(nb,),
        in_specs=[
            pl.BlockSpec((rows, hd), full),
            pl.BlockSpec((block, hd), kv_map),
            pl.BlockSpec((block, hd), kv_map),
            pl.BlockSpec((1, block), own_map),
            pl.BlockSpec((rows, 1), full),
        ],
        out_specs=[
            pl.BlockSpec((rows, 1), full),
            pl.BlockSpec((rows, 1), full),
            pl.BlockSpec((rows, hd), full),
        ],
        scratch_shapes=[
            pltpu.VMEM((rows, 1), jnp.float32),
            pltpu.VMEM((rows, 1), jnp.float32),
            pltpu.VMEM((rows, hd), jnp.float32),
        ],
    )
    flops = 4 * rows * pool * hd
    cost = pl.CostEstimate(flops=flops, transcendentals=rows * pool,
                           bytes_accessed=2 * pool * hd * 2 + pool * 4 + rows * hd * 6)
    m, l, acc = pl.pallas_call(
        functools.partial(_cache_kernel, scale=scale),
        grid_spec=grid_spec,
        out_shape=[
            jax.ShapeDtypeStruct((rows, 1), jnp.float32),
            jax.ShapeDtypeStruct((rows, 1), jnp.float32),
            jax.ShapeDtypeStruct((rows, hd), jnp.float32),
        ],
        compiler_params=pltpu.CompilerParams(dimension_semantics=("arbitrary",)),
        cost_estimate=cost,
    )(live_blocks.reshape(1).astype(jnp.int32), query_rows, cache_keys, cache_values,
      cache_req.reshape(1, pool), row_req.reshape(rows, 1))
    return m[:, 0], l[:, 0], acc


def attend(queries, new_keys, new_values, cache_keys, cache_values, tok_req, cache_req):
    tokens_here = queries.shape[0]
    head_dim = HD
    kv_here = new_keys.shape[1] // head_dim
    group_size = queries.shape[1] // (kv_here * head_dim)
    score_scale = 1.0 / math.sqrt(head_dim)
    row_count = tokens_here * group_size
    grouped = queries.reshape(tokens_here, kv_here, group_size, head_dim)
    row_req = jnp.repeat(tok_req, group_size)
    row_tok = jnp.repeat(jnp.arange(tokens_here, dtype=jnp.int32), group_size)
    pool_size = cache_keys.shape[0]
    block_width = min(key_block, pool_size)
    live_slots = jnp.sum((cache_req >= 0).astype(jnp.int32))
    live_blocks = (live_slots + block_width - 1) // block_width

    def update(carried, block_keys, block_values, visible):
        running_max, denominator, weighted = carried[0]
        query_rows = grouped[:, 0].reshape(row_count, head_dim)
        scores = (
            jnp.einsum("qd,kd->qk", query_rows, block_keys, preferred_element_type=jnp.float32)
            * score_scale
        )
        masked = jnp.where(visible, scores, masked_value)
        new_max = jnp.maximum(running_max, jnp.max(masked, axis=1))
        weights = jnp.where(visible, jnp.exp(masked - new_max[:, None]), 0.0).astype(jnp.bfloat16)
        factor = jnp.exp(running_max - new_max)
        denominator = denominator * factor + jnp.sum(weights.astype(jnp.float32), axis=1)
        weighted = weighted * factor[:, None] + jnp.dot(
            weights, block_values, preferred_element_type=jnp.float32
        )
        renewed = [(new_max, denominator, weighted)]
        return tuple(renewed)

    initial = tuple(
        (
            (
                jnp.full((row_count,), masked_value, jnp.float32),
                jnp.zeros((row_count,), jnp.float32),
                jnp.zeros((row_count, head_dim), jnp.float32),
            )
            for _ in range(kv_here)
        )
    )

    carried = (
        cache_attention(
            grouped[:, 0].reshape(row_count, head_dim), cache_keys, cache_values,
            cache_req, row_req, live_blocks, block_width, score_scale,
        ),
    )
    causal = (tok_req[None, :] == row_req[:, None]) & (
        jnp.arange(tokens_here, dtype=jnp.int32)[None, :] <= row_tok[:, None]
    )
    carried = update(carried, new_keys, new_values, causal)
    per_head = [
        (weighted / denominator[:, None]).reshape(tokens_here, group_size, head_dim)
        for running_max, denominator, weighted in carried
    ]
    return (
        jnp.stack(per_head, axis=1)
        .reshape(tokens_here, kv_here * group_size * head_dim)
        .astype(jnp.bfloat16)
    )


def per_device(
    queries,
    new_keys,
    new_values,
    cache_keys,
    cache_values,
    tok_req,
    cache_req,
    out_weight,
    residual,
    norm_gain,
    gate_weight,
    up_weight,
    down_weight,
):
    swap = [(0, 1), (1, 0)]
    req_count = lax.axis_size("req")
    columns = down_weight.shape[1] // req_count
    down_blocks = down_weight.reshape(down_weight.shape[0], req_count, columns)
    gate_partner = lax.ppermute(gate_weight, "core", swap)
    up_partner = lax.ppermute(up_weight, "core", swap)
    down_partner = lax.ppermute(down_blocks, "core", swap)
    attended = attend(queries, new_keys, new_values, cache_keys, cache_values, tok_req, cache_req)
    partial_out = jnp.dot(
        lax.all_gather(attended, "req", axis=0, tiled=True),
        out_weight,
        preferred_element_type=jnp.float32,
    )
    mixed = lax.psum_scatter(
        partial_out.astype(jnp.bfloat16), ("y", "core"), scatter_dimension=0, tiled=True
    ).astype(jnp.float32)
    stream = (residual.astype(jnp.float32) + mixed).astype(jnp.bfloat16)
    y_count = lax.axis_size("y")
    tokens_out = stream.shape[0]
    side_stream = lax.all_gather(
        lax.all_gather(stream, "req", axis=1, tiled=True), "y", axis=0, tiled=True
    )
    wide_side = side_stream.astype(jnp.float32)
    mean_square = jnp.mean(wide_side * wide_side, axis=1, keepdims=True)
    normed = (wide_side * lax.rsqrt(mean_square + epsilon) * norm_gain[None, :]).astype(
        jnp.bfloat16
    )

    def hidden_of(gate_w, up_w):
        gate = jnp.dot(normed, gate_w, preferred_element_type=jnp.float32)
        up = jnp.dot(normed, up_w, preferred_element_type=jnp.float32)
        hidden = (jax.nn.silu(gate) * up).astype(jnp.bfloat16)
        return hidden.reshape(y_count, tokens_out, hidden.shape[1])

    def down_of(hidden, down_w):
        return jnp.einsum(
            "ysh,hrf->rysf",
            hidden,
            down_w,
            preferred_element_type=jnp.float32,
        )

    product = down_of(hidden_of(gate_weight, up_weight), down_blocks) + down_of(
        hidden_of(gate_partner, up_partner), down_partner
    )
    pieces = product.astype(jnp.bfloat16).reshape(req_count * y_count, tokens_out, columns)
    received = lax.all_to_all(pieces, ("req", "y"), 0, 0, tiled=True)
    summed = jnp.sum(received.astype(jnp.float32), axis=0)
    return (stream.astype(jnp.float32) + summed).astype(jnp.bfloat16)


def solution(mesh):
    req_count, tp_count = mesh.devices.shape
    split = jax.sharding.Mesh(
        mesh.devices.reshape(req_count, tp_count // 2, 2), ("req", "y", "core")
    )
    tp = ("y", "core")
    in_specs = (
        P("req", tp),
        P("req", tp),
        P("req", tp),
        P("req", tp),
        P("req", tp),
        P("req"),
        P("req"),
        P(tp, "req"),
        P(tp, "req"),
        P(),
        P(None, ("req",) + tp),
        P(None, ("req",) + tp),
        P(("req",) + tp, None),
    )
    out_specs = P(tp, "req")
    return jax.shard_map(
        per_device, mesh=split, in_specs=in_specs, out_specs=out_specs, check_vma=False
    )
```

```python
import functools
import math

import jax
import jax.numpy as jnp
from jax import lax
from jax.experimental import pallas as pl
from jax.experimental.pallas import tpu as pltpu
from jax.sharding import PartitionSpec as P


HD = 128


epsilon = 1e-05
masked_value = -1e30
key_block = 1792


def _cache_kernel(live_ref, q_ref, k_ref, v_ref, owner_ref, rowreq_ref, m_out, l_out, acc_out, m_s, l_s, acc_s, *, scale):
    i = pl.program_id(0)

    @pl.when(i == 0)
    def _init():
        m_s[...] = jnp.full(m_s.shape, masked_value, jnp.float32)
        l_s[...] = jnp.zeros(l_s.shape, jnp.float32)
        acc_s[...] = jnp.zeros(acc_s.shape, jnp.float32)

    @pl.when(i < live_ref[0])
    def _step():
        scores = lax.dot_general(q_ref[...], k_ref[...], (((1,), (1,)), ((), ())),
                                 preferred_element_type=jnp.float32) * scale
        visible = owner_ref[...] == rowreq_ref[...]
        masked = jnp.where(visible, scores, masked_value)
        running = m_s[...]
        new_max = jnp.maximum(running, jnp.max(masked, axis=1, keepdims=True))
        weights = jnp.where(visible, jnp.exp(masked - new_max), 0.0).astype(jnp.bfloat16)
        factor = jnp.exp(running - new_max)
        l_s[...] = l_s[...] * factor + jnp.sum(weights.astype(jnp.float32), axis=1, keepdims=True)
        acc_s[...] = acc_s[...] * factor + jnp.dot(weights, v_ref[...], preferred_element_type=jnp.float32)
        m_s[...] = new_max

    @pl.when(i == pl.num_programs(0) - 1)
    def _done():
        m_out[...] = m_s[...]
        l_out[...] = l_s[...]
        acc_out[...] = acc_s[...]


def cache_attention(query_rows, cache_keys, cache_values, cache_req, row_req, live_blocks, block, scale):
    rows, hd = query_rows.shape
    pool = cache_keys.shape[0]
    nb = pool // block

    def kv_map(i, live):
        return (jnp.maximum(jnp.minimum(i, live[0] - 1), 0), 0)

    def own_map(i, live):
        return (0, jnp.maximum(jnp.minimum(i, live[0] - 1), 0))

    full = lambda i, live: (0, 0)
    grid_spec = pltpu.PrefetchScalarGridSpec(
        num_scalar_prefetch=1,
        grid=(nb,),
        in_specs=[
            pl.BlockSpec((rows, hd), full),
            pl.BlockSpec((block, hd), kv_map),
            pl.BlockSpec((block, hd), kv_map),
            pl.BlockSpec((1, block), own_map),
            pl.BlockSpec((rows, 1), full),
        ],
        out_specs=[
            pl.BlockSpec((rows, 1), full),
            pl.BlockSpec((rows, 1), full),
            pl.BlockSpec((rows, hd), full),
        ],
        scratch_shapes=[
            pltpu.VMEM((rows, 1), jnp.float32),
            pltpu.VMEM((rows, 1), jnp.float32),
            pltpu.VMEM((rows, hd), jnp.float32),
        ],
    )
    flops = 4 * rows * pool * hd
    cost = pl.CostEstimate(flops=flops, transcendentals=rows * pool,
                           bytes_accessed=2 * pool * hd * 2 + pool * 4 + rows * hd * 6)
    m, l, acc = pl.pallas_call(
        functools.partial(_cache_kernel, scale=scale),
        grid_spec=grid_spec,
        out_shape=[
            jax.ShapeDtypeStruct((rows, 1), jnp.float32),
            jax.ShapeDtypeStruct((rows, 1), jnp.float32),
            jax.ShapeDtypeStruct((rows, hd), jnp.float32),
        ],
        compiler_params=pltpu.CompilerParams(dimension_semantics=("arbitrary",)),
        cost_estimate=cost,
    )(live_blocks.reshape(1).astype(jnp.int32), query_rows, cache_keys, cache_values,
      cache_req.reshape(1, pool), row_req.reshape(rows, 1))
    return m[:, 0], l[:, 0], acc


def attend(queries, new_keys, new_values, cache_keys, cache_values, tok_req, cache_req):
    tokens_here = queries.shape[0]
    head_dim = HD
    kv_here = new_keys.shape[1] // head_dim
    group_size = queries.shape[1] // (kv_here * head_dim)
    score_scale = 1.0 / math.sqrt(head_dim)
    row_count = tokens_here * group_size
    grouped = queries.reshape(tokens_here, kv_here, group_size, head_dim)
    row_req = jnp.repeat(tok_req, group_size)
    row_tok = jnp.repeat(jnp.arange(tokens_here, dtype=jnp.int32), group_size)
    pool_size = cache_keys.shape[0]
    block_width = min(key_block, pool_size)
    live_slots = jnp.sum((cache_req >= 0).astype(jnp.int32))
    live_blocks = (live_slots + block_width - 1) // block_width

    def update(carried, block_keys, block_values, visible):
        running_max, denominator, weighted = carried[0]
        query_rows = grouped[:, 0].reshape(row_count, head_dim)
        scores = (
            jnp.einsum("qd,kd->qk", query_rows, block_keys, preferred_element_type=jnp.float32)
            * score_scale
        )
        masked = jnp.where(visible, scores, masked_value)
        new_max = jnp.maximum(running_max, jnp.max(masked, axis=1))
        weights = jnp.where(visible, jnp.exp(masked - new_max[:, None]), 0.0).astype(jnp.bfloat16)
        factor = jnp.exp(running_max - new_max)
        denominator = denominator * factor + jnp.sum(weights.astype(jnp.float32), axis=1)
        weighted = weighted * factor[:, None] + jnp.dot(
            weights, block_values, preferred_element_type=jnp.float32
        )
        renewed = [(new_max, denominator, weighted)]
        return tuple(renewed)

    initial = tuple(
        (
            (
                jnp.full((row_count,), masked_value, jnp.float32),
                jnp.zeros((row_count,), jnp.float32),
                jnp.zeros((row_count, head_dim), jnp.float32),
            )
            for _ in range(kv_here)
        )
    )

    carried = (
        cache_attention(
            grouped[:, 0].reshape(row_count, head_dim), cache_keys, cache_values,
            cache_req, row_req, live_blocks, block_width, score_scale,
        ),
    )
    causal = (tok_req[None, :] == row_req[:, None]) & (
        jnp.arange(tokens_here, dtype=jnp.int32)[None, :] <= row_tok[:, None]
    )
    carried = update(carried, new_keys, new_values, causal)
    per_head = [
        (weighted / denominator[:, None]).reshape(tokens_here, group_size, head_dim)
        for running_max, denominator, weighted in carried
    ]
    return (
        jnp.stack(per_head, axis=1)
        .reshape(tokens_here, kv_here * group_size * head_dim)
        .astype(jnp.bfloat16)
    )


def per_device(
    queries,
    new_keys,
    new_values,
    cache_keys,
    cache_values,
    tok_req,
    cache_req,
    out_weight,
    residual,
    norm_gain,
    gate_weight,
    up_weight,
    down_weight,
):
    swap = [(0, 1), (1, 0)]
    req_count = lax.axis_size("req")
    y_count = lax.axis_size("y")
    core_count = lax.axis_size("core")
    tokens_out, columns = residual.shape
    gate_partner = lax.ppermute(gate_weight, "core", swap)
    up_partner = lax.ppermute(up_weight, "core", swap)
    down_partner = lax.ppermute(down_weight, "core", swap)
    attended = attend(queries, new_keys, new_values, cache_keys, cache_values, tok_req, cache_req)
    partial_out = jnp.dot(
        lax.all_gather(attended, "req", axis=0, tiled=True),
        out_weight,
        preferred_element_type=jnp.float32,
    )
    core = lax.axis_index("core")
    first_row = (lax.axis_index("y") * core_count + core) * tokens_out
    own_rows = lax.dynamic_slice_in_dim(partial_out, first_row, tokens_out, 0)
    partial_out = lax.dynamic_update_slice_in_dim(
        partial_out, own_rows + residual.astype(jnp.float32), first_row, 0
    )
    stream_rows = lax.psum(partial_out, ("y", "core")).astype(jnp.bfloat16)
    stream = lax.dynamic_slice_in_dim(stream_rows, first_row, tokens_out, 0)
    side_rows = lax.dynamic_index_in_dim(
        stream_rows.reshape(y_count, core_count, tokens_out, columns), core, 1, keepdims=False
    ).reshape(y_count * tokens_out, columns)
    side_stream = lax.all_gather(side_rows, "req", axis=1, tiled=True)
    wide_side = side_stream.astype(jnp.float32)
    mean_square = jnp.mean(wide_side * wide_side, axis=1, keepdims=True)
    normed = (wide_side * lax.rsqrt(mean_square + epsilon) * norm_gain[None, :]).astype(
        jnp.bfloat16
    )

    def hidden_of(gate_w, up_w):
        gate = jnp.dot(normed, gate_w, preferred_element_type=jnp.float32)
        up = jnp.dot(normed, up_w, preferred_element_type=jnp.float32)
        hidden = (jax.nn.silu(gate) * up).astype(jnp.bfloat16)
        return hidden.reshape(y_count, tokens_out, hidden.shape[1])

    def down_of(hidden, down_w):
        return jnp.einsum(
            "ysh,hrf->rysf",
            hidden,
            down_w,
            preferred_element_type=jnp.float32,
        )

    def blocks_of(down_w):
        return down_w.reshape(down_w.shape[0], req_count, columns)

    product = down_of(hidden_of(gate_weight, up_weight), blocks_of(down_weight)) + down_of(
        hidden_of(gate_partner, up_partner), blocks_of(down_partner)
    )
    pieces = product.astype(jnp.bfloat16).reshape(req_count * y_count, tokens_out, columns)
    received = lax.all_to_all(pieces, ("req", "y"), 0, 0, tiled=True)
    summed = jnp.sum(received.astype(jnp.float32), axis=0)
    return (stream.astype(jnp.float32) + summed).astype(jnp.bfloat16)


def solution(mesh):
    req_count, tp_count = mesh.devices.shape
    split = jax.sharding.Mesh(
        mesh.devices.reshape(req_count, tp_count // 2, 2), ("req", "y", "core")
    )
    tp = ("y", "core")
    in_specs = (
        P("req", tp),
        P("req", tp),
        P("req", tp),
        P("req", tp),
        P("req", tp),
        P("req"),
        P("req"),
        P(tp, "req"),
        P(tp, "req"),
        P(),
        P(None, ("req",) + tp),
        P(None, ("req",) + tp),
        P(("req",) + tp, None),
    )
    out_specs = P(tp, "req")
    return jax.shard_map(
        per_device, mesh=split, in_specs=in_specs, out_specs=out_specs, check_vma=False
    )
```

```python
import functools
import math

import jax
import jax.numpy as jnp
from jax import lax
from jax.experimental import pallas as pl
from jax.experimental.pallas import tpu as pltpu
from jax.sharding import PartitionSpec as P


HD = 128


epsilon = 1e-05
masked_value = -1e30
key_block = 1792


def _cache_kernel(live_ref, q_ref, k_ref, v_ref, owner_ref, rowreq_ref, m_out, l_out, acc_out, m_s, l_s, acc_s, *, scale):
    i = pl.program_id(0)

    @pl.when(i == 0)
    def _init():
        m_s[...] = jnp.full(m_s.shape, masked_value, jnp.float32)
        l_s[...] = jnp.zeros(l_s.shape, jnp.float32)
        acc_s[...] = jnp.zeros(acc_s.shape, jnp.float32)

    @pl.when(i < live_ref[0])
    def _step():
        scores = lax.dot_general(q_ref[...], k_ref[...], (((1,), (1,)), ((), ())),
                                 preferred_element_type=jnp.float32) * scale
        visible = owner_ref[...] == rowreq_ref[...]
        masked = jnp.where(visible, scores, masked_value)
        running = m_s[...]
        new_max = jnp.maximum(running, jnp.max(masked, axis=1, keepdims=True))
        weights = jnp.where(visible, jnp.exp(masked - new_max), 0.0).astype(jnp.bfloat16)
        factor = jnp.exp(running - new_max)
        l_s[...] = l_s[...] * factor + jnp.sum(weights.astype(jnp.float32), axis=1, keepdims=True)
        acc_s[...] = acc_s[...] * factor + jnp.dot(weights, v_ref[...], preferred_element_type=jnp.float32)
        m_s[...] = new_max

    @pl.when(i == pl.num_programs(0) - 1)
    def _done():
        m_out[...] = m_s[...]
        l_out[...] = l_s[...]
        acc_out[...] = acc_s[...]


def cache_attention(query_rows, cache_keys, cache_values, cache_req, row_req, live_blocks, block, scale):
    rows, hd = query_rows.shape
    pool = cache_keys.shape[0]
    nb = pool // block

    def kv_map(i, live):
        return (jnp.maximum(jnp.minimum(i, live[0] - 1), 0), 0)

    def own_map(i, live):
        return (0, jnp.maximum(jnp.minimum(i, live[0] - 1), 0))

    full = lambda i, live: (0, 0)
    grid_spec = pltpu.PrefetchScalarGridSpec(
        num_scalar_prefetch=1,
        grid=(nb,),
        in_specs=[
            pl.BlockSpec((rows, hd), full),
            pl.BlockSpec((block, hd), kv_map),
            pl.BlockSpec((block, hd), kv_map),
            pl.BlockSpec((1, block), own_map),
            pl.BlockSpec((rows, 1), full),
        ],
        out_specs=[
            pl.BlockSpec((rows, 1), full),
            pl.BlockSpec((rows, 1), full),
            pl.BlockSpec((rows, hd), full),
        ],
        scratch_shapes=[
            pltpu.VMEM((rows, 1), jnp.float32),
            pltpu.VMEM((rows, 1), jnp.float32),
            pltpu.VMEM((rows, hd), jnp.float32),
        ],
    )
    flops = 4 * rows * pool * hd
    cost = pl.CostEstimate(flops=flops, transcendentals=rows * pool,
                           bytes_accessed=2 * pool * hd * 2 + pool * 4 + rows * hd * 6)
    m, l, acc = pl.pallas_call(
        functools.partial(_cache_kernel, scale=scale),
        grid_spec=grid_spec,
        out_shape=[
            jax.ShapeDtypeStruct((rows, 1), jnp.float32),
            jax.ShapeDtypeStruct((rows, 1), jnp.float32),
            jax.ShapeDtypeStruct((rows, hd), jnp.float32),
        ],
        compiler_params=pltpu.CompilerParams(dimension_semantics=("arbitrary",)),
        cost_estimate=cost,
    )(live_blocks.reshape(1).astype(jnp.int32), query_rows, cache_keys, cache_values,
      cache_req.reshape(1, pool), row_req.reshape(rows, 1))
    return m[:, 0], l[:, 0], acc


def attend(queries, new_keys, new_values, cache_keys, cache_values, tok_req, cache_req):
    tokens_here = queries.shape[0]
    head_dim = HD
    kv_here = new_keys.shape[1] // head_dim
    group_size = queries.shape[1] // (kv_here * head_dim)
    score_scale = 1.0 / math.sqrt(head_dim)
    row_count = tokens_here * group_size
    grouped = queries.reshape(tokens_here, kv_here, group_size, head_dim)
    row_req = jnp.repeat(tok_req, group_size)
    row_tok = jnp.repeat(jnp.arange(tokens_here, dtype=jnp.int32), group_size)
    pool_size = cache_keys.shape[0]
    block_width = min(key_block, pool_size)
    live_slots = jnp.sum((cache_req >= 0).astype(jnp.int32))
    live_blocks = (live_slots + block_width - 1) // block_width

    def update(carried, block_keys, block_values, visible):
        running_max, denominator, weighted = carried[0]
        query_rows = grouped[:, 0].reshape(row_count, head_dim)
        scores = (
            jnp.einsum("qd,kd->qk", query_rows, block_keys, preferred_element_type=jnp.float32)
            * score_scale
        )
        masked = jnp.where(visible, scores, masked_value)
        new_max = jnp.maximum(running_max, jnp.max(masked, axis=1))
        weights = jnp.where(visible, jnp.exp(masked - new_max[:, None]), 0.0).astype(jnp.bfloat16)
        factor = jnp.exp(running_max - new_max)
        denominator = denominator * factor + jnp.sum(weights.astype(jnp.float32), axis=1)
        weighted = weighted * factor[:, None] + jnp.dot(
            weights, block_values, preferred_element_type=jnp.float32
        )
        renewed = [(new_max, denominator, weighted)]
        return tuple(renewed)

    initial = tuple(
        (
            (
                jnp.full((row_count,), masked_value, jnp.float32),
                jnp.zeros((row_count,), jnp.float32),
                jnp.zeros((row_count, head_dim), jnp.float32),
            )
            for _ in range(kv_here)
        )
    )

    carried = (
        cache_attention(
            grouped[:, 0].reshape(row_count, head_dim), cache_keys, cache_values,
            cache_req, row_req, live_blocks, block_width, score_scale,
        ),
    )
    causal = (tok_req[None, :] == row_req[:, None]) & (
        jnp.arange(tokens_here, dtype=jnp.int32)[None, :] <= row_tok[:, None]
    )
    carried = update(carried, new_keys, new_values, causal)
    per_head = [
        (weighted / denominator[:, None]).reshape(tokens_here, group_size, head_dim)
        for running_max, denominator, weighted in carried
    ]
    return (
        jnp.stack(per_head, axis=1)
        .reshape(tokens_here, kv_here * group_size * head_dim)
        .astype(jnp.bfloat16)
    )


def per_device(
    queries,
    new_keys,
    new_values,
    cache_keys,
    cache_values,
    tok_req,
    cache_req,
    out_weight,
    residual,
    norm_gain,
    gate_weight,
    up_weight,
    down_weight,
):
    swap = [(0, 1), (1, 0)]
    req_count = lax.axis_size("req")
    y_count = lax.axis_size("y")
    core_count = lax.axis_size("core")
    tokens_out, columns = residual.shape
    gate_partner = lax.ppermute(gate_weight, "core", swap)
    up_partner = lax.ppermute(up_weight, "core", swap)
    down_partner = lax.ppermute(down_weight, "core", swap)
    attended = attend(queries, new_keys, new_values, cache_keys, cache_values, tok_req, cache_req)
    partial_out = jnp.dot(
        lax.all_gather(attended, "req", axis=0, tiled=True),
        out_weight,
        preferred_element_type=jnp.float32,
    )
    core = lax.axis_index("core")
    first_row = (lax.axis_index("y") * core_count + core) * tokens_out
    own_rows = lax.dynamic_slice_in_dim(partial_out, first_row, tokens_out, 0)
    partial_out = lax.dynamic_update_slice_in_dim(
        partial_out, own_rows + residual.astype(jnp.float32), first_row, 0
    )
    parts = partial_out.reshape(y_count, core_count, tokens_out, columns)
    mine = lax.dynamic_index_in_dim(parts, core, 1, keepdims=False)
    theirs = lax.dynamic_index_in_dim(parts, 1 - core, 1, keepdims=False)
    side_partial = mine + lax.ppermute(theirs, "core", swap)
    side_rows = lax.psum(side_partial, "y").astype(jnp.bfloat16)
    stream = lax.dynamic_index_in_dim(side_rows, lax.axis_index("y"), 0, keepdims=False)
    side_rows = side_rows.reshape(y_count * tokens_out, columns)
    side_stream = lax.all_gather(side_rows, "req", axis=1, tiled=True)
    wide_side = side_stream.astype(jnp.float32)
    mean_square = jnp.mean(wide_side * wide_side, axis=1, keepdims=True)
    normed = (wide_side * lax.rsqrt(mean_square + epsilon) * norm_gain[None, :]).astype(
        jnp.bfloat16
    )

    def hidden_of(gate_w, up_w):
        gate = jnp.dot(normed, gate_w, preferred_element_type=jnp.float32)
        up = jnp.dot(normed, up_w, preferred_element_type=jnp.float32)
        hidden = (jax.nn.silu(gate) * up).astype(jnp.bfloat16)
        return hidden.reshape(y_count, tokens_out, hidden.shape[1])

    def down_of(hidden, down_w):
        return jnp.einsum(
            "ysh,hrf->rysf",
            hidden,
            down_w,
            preferred_element_type=jnp.float32,
        )

    def blocks_of(down_w):
        return down_w.reshape(down_w.shape[0], req_count, columns)

    product = down_of(hidden_of(gate_weight, up_weight), blocks_of(down_weight)) + down_of(
        hidden_of(gate_partner, up_partner), blocks_of(down_partner)
    )
    pieces = product.astype(jnp.bfloat16).reshape(req_count * y_count, tokens_out, columns)
    received = lax.all_to_all(pieces, ("req", "y"), 0, 0, tiled=True)
    summed = jnp.sum(received.astype(jnp.float32), axis=0)
    return (stream.astype(jnp.float32) + summed).astype(jnp.bfloat16)


def solution(mesh):
    req_count, tp_count = mesh.devices.shape
    split = jax.sharding.Mesh(
        mesh.devices.reshape(req_count, tp_count // 2, 2), ("req", "y", "core")
    )
    tp = ("y", "core")
    in_specs = (
        P("req", tp),
        P("req", tp),
        P("req", tp),
        P("req", tp),
        P("req", tp),
        P("req"),
        P("req"),
        P(tp, "req"),
        P(tp, "req"),
        P(),
        P(None, ("req",) + tp),
        P(None, ("req",) + tp),
        P(("req",) + tp, None),
    )
    out_specs = P(tp, "req")
    return jax.shard_map(
        per_device, mesh=split, in_specs=in_specs, out_specs=out_specs, check_vma=False
    )
```

```python
import functools
import math

import jax
import jax.numpy as jnp
from jax import lax
from jax.experimental import pallas as pl
from jax.experimental.pallas import tpu as pltpu
from jax.sharding import PartitionSpec as P


HD = 128


epsilon = 1e-05
masked_value = -1e30
key_block = 1792


def _cache_kernel(live_ref, q_ref, k_ref, v_ref, owner_ref, rowreq_ref, m_out, l_out, acc_out, m_s, l_s, acc_s, *, scale):
    i = pl.program_id(0)

    @pl.when(i == 0)
    def _init():
        m_s[...] = jnp.full(m_s.shape, masked_value, jnp.float32)
        l_s[...] = jnp.zeros(l_s.shape, jnp.float32)
        acc_s[...] = jnp.zeros(acc_s.shape, jnp.float32)

    @pl.when(i < live_ref[0])
    def _step():
        scores = lax.dot_general(q_ref[...], k_ref[...], (((1,), (1,)), ((), ())),
                                 preferred_element_type=jnp.float32) * scale
        visible = owner_ref[...] == rowreq_ref[...]
        masked = jnp.where(visible, scores, masked_value)
        running = m_s[...]
        new_max = jnp.maximum(running, jnp.max(masked, axis=1, keepdims=True))
        weights = jnp.where(visible, jnp.exp(masked - new_max), 0.0).astype(jnp.bfloat16)
        factor = jnp.exp(running - new_max)
        l_s[...] = l_s[...] * factor + jnp.sum(weights.astype(jnp.float32), axis=1, keepdims=True)
        acc_s[...] = acc_s[...] * factor + jnp.dot(weights, v_ref[...], preferred_element_type=jnp.float32)
        m_s[...] = new_max

    @pl.when(i == pl.num_programs(0) - 1)
    def _done():
        m_out[...] = m_s[...]
        l_out[...] = l_s[...]
        acc_out[...] = acc_s[...]


def cache_attention(query_rows, cache_keys, cache_values, cache_req, row_req, live_blocks, block, scale):
    rows, hd = query_rows.shape
    pool = cache_keys.shape[0]
    nb = pool // block

    def kv_map(i, live):
        return (jnp.maximum(jnp.minimum(i, live[0] - 1), 0), 0)

    def own_map(i, live):
        return (0, jnp.maximum(jnp.minimum(i, live[0] - 1), 0))

    full = lambda i, live: (0, 0)
    grid_spec = pltpu.PrefetchScalarGridSpec(
        num_scalar_prefetch=1,
        grid=(nb,),
        in_specs=[
            pl.BlockSpec((rows, hd), full),
            pl.BlockSpec((block, hd), kv_map),
            pl.BlockSpec((block, hd), kv_map),
            pl.BlockSpec((1, block), own_map),
            pl.BlockSpec((rows, 1), full),
        ],
        out_specs=[
            pl.BlockSpec((rows, 1), full),
            pl.BlockSpec((rows, 1), full),
            pl.BlockSpec((rows, hd), full),
        ],
        scratch_shapes=[
            pltpu.VMEM((rows, 1), jnp.float32),
            pltpu.VMEM((rows, 1), jnp.float32),
            pltpu.VMEM((rows, hd), jnp.float32),
        ],
    )
    flops = 4 * rows * pool * hd
    cost = pl.CostEstimate(flops=flops, transcendentals=rows * pool,
                           bytes_accessed=2 * pool * hd * 2 + pool * 4 + rows * hd * 6)
    m, l, acc = pl.pallas_call(
        functools.partial(_cache_kernel, scale=scale),
        grid_spec=grid_spec,
        out_shape=[
            jax.ShapeDtypeStruct((rows, 1), jnp.float32),
            jax.ShapeDtypeStruct((rows, 1), jnp.float32),
            jax.ShapeDtypeStruct((rows, hd), jnp.float32),
        ],
        compiler_params=pltpu.CompilerParams(dimension_semantics=("arbitrary",)),
        cost_estimate=cost,
    )(live_blocks.reshape(1).astype(jnp.int32), query_rows, cache_keys, cache_values,
      cache_req.reshape(1, pool), row_req.reshape(rows, 1))
    return m[:, 0], l[:, 0], acc


def attend(queries, new_keys, new_values, cache_keys, cache_values, tok_req, cache_req):
    tokens_here = queries.shape[0]
    head_dim = HD
    kv_here = new_keys.shape[1] // head_dim
    group_size = queries.shape[1] // (kv_here * head_dim)
    score_scale = 1.0 / math.sqrt(head_dim)
    row_count = tokens_here * group_size
    grouped = queries.reshape(tokens_here, kv_here, group_size, head_dim)
    row_req = jnp.repeat(tok_req, group_size)
    row_tok = jnp.repeat(jnp.arange(tokens_here, dtype=jnp.int32), group_size)
    pool_size = cache_keys.shape[0]
    block_width = min(key_block, pool_size)
    live_slots = jnp.sum((cache_req >= 0).astype(jnp.int32))
    live_blocks = (live_slots + block_width - 1) // block_width

    def update(carried, block_keys, block_values, visible):
        running_max, denominator, weighted = carried[0]
        query_rows = grouped[:, 0].reshape(row_count, head_dim)
        scores = (
            jnp.einsum("qd,kd->qk", query_rows, block_keys, preferred_element_type=jnp.float32)
            * score_scale
        )
        masked = jnp.where(visible, scores, masked_value)
        new_max = jnp.maximum(running_max, jnp.max(masked, axis=1))
        weights = jnp.where(visible, jnp.exp(masked - new_max[:, None]), 0.0).astype(jnp.bfloat16)
        factor = jnp.exp(running_max - new_max)
        denominator = denominator * factor + jnp.sum(weights.astype(jnp.float32), axis=1)
        weighted = weighted * factor[:, None] + jnp.dot(
            weights, block_values, preferred_element_type=jnp.float32
        )
        renewed = [(new_max, denominator, weighted)]
        return tuple(renewed)

    initial = tuple(
        (
            (
                jnp.full((row_count,), masked_value, jnp.float32),
                jnp.zeros((row_count,), jnp.float32),
                jnp.zeros((row_count, head_dim), jnp.float32),
            )
            for _ in range(kv_here)
        )
    )

    carried = (
        cache_attention(
            grouped[:, 0].reshape(row_count, head_dim), cache_keys, cache_values,
            cache_req, row_req, live_blocks, block_width, score_scale,
        ),
    )
    causal = (tok_req[None, :] == row_req[:, None]) & (
        jnp.arange(tokens_here, dtype=jnp.int32)[None, :] <= row_tok[:, None]
    )
    carried = update(carried, new_keys, new_values, causal)
    per_head = [
        (weighted / denominator[:, None]).reshape(tokens_here, group_size, head_dim)
        for running_max, denominator, weighted in carried
    ]
    return (
        jnp.stack(per_head, axis=1)
        .reshape(tokens_here, kv_here * group_size * head_dim)
        .astype(jnp.bfloat16)
    )


def per_device(
    queries,
    new_keys,
    new_values,
    cache_keys,
    cache_values,
    tok_req,
    cache_req,
    out_weight,
    residual,
    norm_gain,
    gate_weight,
    up_weight,
    down_weight,
):
    swap = [(0, 1), (1, 0)]
    req_count = lax.axis_size("req")
    y_count = lax.axis_size("y")
    core_count = lax.axis_size("core")
    tokens_out, columns = residual.shape
    gate_partner = lax.ppermute(gate_weight, "core", swap)
    up_partner = lax.ppermute(up_weight, "core", swap)
    down_partner = lax.ppermute(down_weight, "core", swap)
    attended = attend(queries, new_keys, new_values, cache_keys, cache_values, tok_req, cache_req)
    partial_out = jnp.dot(
        lax.all_gather(attended, "req", axis=0, tiled=True),
        out_weight,
        preferred_element_type=jnp.float32,
    )
    core = lax.axis_index("core")
    first_row = (lax.axis_index("y") * core_count + core) * tokens_out
    own_rows = lax.dynamic_slice_in_dim(partial_out, first_row, tokens_out, 0)
    partial_out = lax.dynamic_update_slice_in_dim(
        partial_out, own_rows + residual.astype(jnp.float32), first_row, 0
    )
    parts = partial_out.reshape(y_count, core_count, tokens_out, columns)
    mine = lax.dynamic_index_in_dim(parts, core, 1, keepdims=False)
    theirs = lax.dynamic_index_in_dim(parts, 1 - core, 1, keepdims=False)
    side_partial = mine + lax.ppermute(theirs, "core", swap)
    side_rows = lax.psum(side_partial, "y").astype(jnp.bfloat16)
    stream = lax.dynamic_index_in_dim(side_rows, lax.axis_index("y"), 0, keepdims=False)
    side_rows = side_rows.reshape(y_count * tokens_out, columns)
    side_stream = lax.all_gather(side_rows, "req", axis=1, tiled=True)
    wide_side = side_stream.astype(jnp.float32)
    mean_square = jnp.mean(wide_side * wide_side, axis=1, keepdims=True)
    normed = (wide_side * lax.rsqrt(mean_square + epsilon) * norm_gain[None, :]).astype(
        jnp.bfloat16
    )

    normed_blocks = normed.reshape(y_count, tokens_out, normed.shape[1])

    def hidden_of(rows, gate_w, up_w):
        gate = jnp.dot(rows, gate_w, preferred_element_type=jnp.float32)
        up = jnp.dot(rows, up_w, preferred_element_type=jnp.float32)
        return (jax.nn.silu(gate) * up).astype(jnp.bfloat16)

    def down_of(hidden, down_w):
        return jnp.einsum(
            "ysh,hrf->rysf",
            hidden.reshape(y_count, -1, hidden.shape[1]),
            down_w.reshape(down_w.shape[0], req_count, columns),
            preferred_element_type=jnp.float32,
        )

    halves = []
    half = tokens_out // 2
    for first in range(0, tokens_out, half):
        rows = normed_blocks[:, first : first + half].reshape(y_count * half, -1)
        product = down_of(hidden_of(rows, gate_weight, up_weight), down_weight) + down_of(
            hidden_of(rows, gate_partner, up_partner), down_partner
        )
        pieces = product.astype(jnp.bfloat16).reshape(req_count * y_count, half, columns)
        received = lax.all_to_all(pieces, ("req", "y"), 0, 0, tiled=True)
        halves.append(jnp.sum(received.astype(jnp.float32), axis=0))
    summed = jnp.concatenate(halves, axis=0)
    return (stream.astype(jnp.float32) + summed).astype(jnp.bfloat16)


def solution(mesh):
    req_count, tp_count = mesh.devices.shape
    split = jax.sharding.Mesh(
        mesh.devices.reshape(req_count, tp_count // 2, 2), ("req", "y", "core")
    )
    tp = ("y", "core")
    in_specs = (
        P("req", tp),
        P("req", tp),
        P("req", tp),
        P("req", tp),
        P("req", tp),
        P("req"),
        P("req"),
        P(tp, "req"),
        P(tp, "req"),
        P(),
        P(None, ("req",) + tp),
        P(None, ("req",) + tp),
        P(("req",) + tp, None),
    )
    out_specs = P(tp, "req")
    return jax.shard_map(
        per_device, mesh=split, in_specs=in_specs, out_specs=out_specs, check_vma=False
    )
```

```python
import functools
import math

import jax
import jax.numpy as jnp
from jax import lax
from jax.experimental import pallas as pl
from jax.experimental.pallas import tpu as pltpu
from jax.sharding import PartitionSpec as P


HD = 128


epsilon = 1e-05
masked_value = -1e30
key_block = 1792


def _cache_kernel(live_ref, q_ref, k_ref, v_ref, owner_ref, rowreq_ref, m_out, l_out, acc_out, m_s, l_s, acc_s, *, scale):
    i = pl.program_id(0)

    @pl.when(i == 0)
    def _init():
        m_s[...] = jnp.full(m_s.shape, masked_value, jnp.float32)
        l_s[...] = jnp.zeros(l_s.shape, jnp.float32)
        acc_s[...] = jnp.zeros(acc_s.shape, jnp.float32)

    @pl.when(i < live_ref[0])
    def _step():
        scores = lax.dot_general(q_ref[...], k_ref[...], (((1,), (1,)), ((), ())),
                                 preferred_element_type=jnp.float32) * scale
        visible = owner_ref[...] == rowreq_ref[...]
        masked = jnp.where(visible, scores, masked_value)
        running = m_s[...]
        new_max = jnp.maximum(running, jnp.max(masked, axis=1, keepdims=True))
        weights = jnp.where(visible, jnp.exp(masked - new_max), 0.0).astype(jnp.bfloat16)
        factor = jnp.exp(running - new_max)
        l_s[...] = l_s[...] * factor + jnp.sum(weights.astype(jnp.float32), axis=1, keepdims=True)
        acc_s[...] = acc_s[...] * factor + jnp.dot(weights, v_ref[...], preferred_element_type=jnp.float32)
        m_s[...] = new_max

    @pl.when(i == pl.num_programs(0) - 1)
    def _done():
        m_out[...] = m_s[...]
        l_out[...] = l_s[...]
        acc_out[...] = acc_s[...]


def cache_attention(query_rows, cache_keys, cache_values, cache_req, row_req, live_blocks, block, scale):
    rows, hd = query_rows.shape
    pool = cache_keys.shape[0]
    nb = pool // block

    def kv_map(i, live):
        return (jnp.maximum(jnp.minimum(i, live[0] - 1), 0), 0)

    def own_map(i, live):
        return (0, jnp.maximum(jnp.minimum(i, live[0] - 1), 0))

    full = lambda i, live: (0, 0)
    grid_spec = pltpu.PrefetchScalarGridSpec(
        num_scalar_prefetch=1,
        grid=(nb,),
        in_specs=[
            pl.BlockSpec((rows, hd), full),
            pl.BlockSpec((block, hd), kv_map),
            pl.BlockSpec((block, hd), kv_map),
            pl.BlockSpec((1, block), own_map),
            pl.BlockSpec((rows, 1), full),
        ],
        out_specs=[
            pl.BlockSpec((rows, 1), full),
            pl.BlockSpec((rows, 1), full),
            pl.BlockSpec((rows, hd), full),
        ],
        scratch_shapes=[
            pltpu.VMEM((rows, 1), jnp.float32),
            pltpu.VMEM((rows, 1), jnp.float32),
            pltpu.VMEM((rows, hd), jnp.float32),
        ],
    )
    flops = 4 * rows * pool * hd
    cost = pl.CostEstimate(flops=flops, transcendentals=rows * pool,
                           bytes_accessed=2 * pool * hd * 2 + pool * 4 + rows * hd * 6)
    m, l, acc = pl.pallas_call(
        functools.partial(_cache_kernel, scale=scale),
        grid_spec=grid_spec,
        out_shape=[
            jax.ShapeDtypeStruct((rows, 1), jnp.float32),
            jax.ShapeDtypeStruct((rows, 1), jnp.float32),
            jax.ShapeDtypeStruct((rows, hd), jnp.float32),
        ],
        compiler_params=pltpu.CompilerParams(dimension_semantics=("arbitrary",)),
        cost_estimate=cost,
    )(live_blocks.reshape(1).astype(jnp.int32), query_rows, cache_keys, cache_values,
      cache_req.reshape(1, pool), row_req.reshape(rows, 1))
    return m[:, 0], l[:, 0], acc


def attend(queries, new_keys, new_values, cache_keys, cache_values, tok_req, cache_req):
    tokens_here = queries.shape[0]
    head_dim = HD
    kv_here = new_keys.shape[1] // head_dim
    group_size = queries.shape[1] // (kv_here * head_dim)
    score_scale = 1.0 / math.sqrt(head_dim)
    row_count = tokens_here * group_size
    grouped = queries.reshape(tokens_here, kv_here, group_size, head_dim)
    row_req = jnp.repeat(tok_req, group_size)
    row_tok = jnp.repeat(jnp.arange(tokens_here, dtype=jnp.int32), group_size)
    pool_size = cache_keys.shape[0]
    block_width = min(key_block, pool_size)
    live_slots = jnp.sum((cache_req >= 0).astype(jnp.int32))
    live_blocks = (live_slots + block_width - 1) // block_width

    def update(carried, block_keys, block_values, visible):
        running_max, denominator, weighted = carried[0]
        query_rows = grouped[:, 0].reshape(row_count, head_dim)
        scores = (
            jnp.einsum("qd,kd->qk", query_rows, block_keys, preferred_element_type=jnp.float32)
            * score_scale
        )
        masked = jnp.where(visible, scores, masked_value)
        new_max = jnp.maximum(running_max, jnp.max(masked, axis=1))
        weights = jnp.where(visible, jnp.exp(masked - new_max[:, None]), 0.0).astype(jnp.bfloat16)
        factor = jnp.exp(running_max - new_max)
        denominator = denominator * factor + jnp.sum(weights.astype(jnp.float32), axis=1)
        weighted = weighted * factor[:, None] + jnp.dot(
            weights, block_values, preferred_element_type=jnp.float32
        )
        renewed = [(new_max, denominator, weighted)]
        return tuple(renewed)

    initial = tuple(
        (
            (
                jnp.full((row_count,), masked_value, jnp.float32),
                jnp.zeros((row_count,), jnp.float32),
                jnp.zeros((row_count, head_dim), jnp.float32),
            )
            for _ in range(kv_here)
        )
    )

    carried = (
        cache_attention(
            grouped[:, 0].reshape(row_count, head_dim), cache_keys, cache_values,
            cache_req, row_req, live_blocks, block_width, score_scale,
        ),
    )
    causal = (tok_req[None, :] == row_req[:, None]) & (
        jnp.arange(tokens_here, dtype=jnp.int32)[None, :] <= row_tok[:, None]
    )
    carried = update(carried, new_keys, new_values, causal)
    per_head = [
        (weighted / denominator[:, None]).reshape(tokens_here, group_size, head_dim)
        for running_max, denominator, weighted in carried
    ]
    return (
        jnp.stack(per_head, axis=1)
        .reshape(tokens_here, kv_here * group_size * head_dim)
        .astype(jnp.bfloat16)
    )


def per_device(
    queries,
    new_keys,
    new_values,
    cache_keys,
    cache_values,
    tok_req,
    cache_req,
    out_weight,
    residual,
    norm_gain,
    gate_weight,
    up_weight,
    down_weight,
):
    swap = [(0, 1), (1, 0)]
    req_count = lax.axis_size("req")
    y_count = lax.axis_size("y")
    core_count = lax.axis_size("core")
    tokens_out, columns = residual.shape
    gate_partner = lax.ppermute(gate_weight, "core", swap)
    up_partner = lax.ppermute(up_weight, "core", swap)
    down_partner = lax.ppermute(down_weight, "core", swap)
    attended = attend(queries, new_keys, new_values, cache_keys, cache_values, tok_req, cache_req)
    shifted = [attended] + [
        lax.ppermute(attended, "req", [(j, (j + k) % req_count) for j in range(req_count)])
        for k in range(1, req_count)
    ]
    by_distance = jnp.stack(shifted)
    order = (lax.axis_index("req") - jnp.arange(req_count, dtype=jnp.int32)) % req_count
    all_groups = jnp.take(by_distance, order, axis=0).reshape(-1, attended.shape[1])
    partial_out = jnp.dot(
        all_groups,
        out_weight,
        preferred_element_type=jnp.float32,
    )
    core = lax.axis_index("core")
    first_row = (lax.axis_index("y") * core_count + core) * tokens_out
    own_rows = lax.dynamic_slice_in_dim(partial_out, first_row, tokens_out, 0)
    partial_out = lax.dynamic_update_slice_in_dim(
        partial_out, own_rows + residual.astype(jnp.float32), first_row, 0
    )
    parts = partial_out.reshape(y_count, core_count, tokens_out, columns)
    mine = lax.dynamic_index_in_dim(parts, core, 1, keepdims=False)
    theirs = lax.dynamic_index_in_dim(parts, 1 - core, 1, keepdims=False)
    side_partial = mine + lax.ppermute(theirs, "core", swap)
    side_rows = lax.psum(side_partial, "y").astype(jnp.bfloat16)
    stream = lax.dynamic_index_in_dim(side_rows, lax.axis_index("y"), 0, keepdims=False)
    side_rows = side_rows.reshape(y_count * tokens_out, columns)
    side_stream = lax.all_gather(side_rows, "req", axis=1, tiled=True)
    wide_side = side_stream.astype(jnp.float32)
    mean_square = jnp.mean(wide_side * wide_side, axis=1, keepdims=True)
    normed = (wide_side * lax.rsqrt(mean_square + epsilon) * norm_gain[None, :]).astype(
        jnp.bfloat16
    )

    def hidden_of(gate_w, up_w):
        gate = jnp.dot(normed, gate_w, preferred_element_type=jnp.float32)
        up = jnp.dot(normed, up_w, preferred_element_type=jnp.float32)
        hidden = (jax.nn.silu(gate) * up).astype(jnp.bfloat16)
        return hidden.reshape(y_count, tokens_out, hidden.shape[1])

    def down_of(hidden, down_w):
        return jnp.einsum(
            "ysh,hrf->rysf",
            hidden,
            down_w,
            preferred_element_type=jnp.float32,
        )

    def blocks_of(down_w):
        return down_w.reshape(down_w.shape[0], req_count, columns)

    product = down_of(hidden_of(gate_weight, up_weight), blocks_of(down_weight)) + down_of(
        hidden_of(gate_partner, up_partner), blocks_of(down_partner)
    )
    pieces = product.astype(jnp.bfloat16).reshape(req_count * y_count, tokens_out, columns)
    received = lax.all_to_all(pieces, ("req", "y"), 0, 0, tiled=True)
    summed = jnp.sum(received.astype(jnp.float32), axis=0)
    return (stream.astype(jnp.float32) + summed).astype(jnp.bfloat16)


def solution(mesh):
    req_count, tp_count = mesh.devices.shape
    split = jax.sharding.Mesh(
        mesh.devices.reshape(req_count, tp_count // 2, 2), ("req", "y", "core")
    )
    tp = ("y", "core")
    in_specs = (
        P("req", tp),
        P("req", tp),
        P("req", tp),
        P("req", tp),
        P("req", tp),
        P("req"),
        P("req"),
        P(tp, "req"),
        P(tp, "req"),
        P(),
        P(None, ("req",) + tp),
        P(None, ("req",) + tp),
        P(("req",) + tp, None),
    )
    out_specs = P(tp, "req")
    return jax.shard_map(
        per_device, mesh=split, in_specs=in_specs, out_specs=out_specs, check_vma=False
    )
```

```python
import functools
import math

import jax
import jax.numpy as jnp
from jax import lax
from jax.experimental import pallas as pl
from jax.experimental.pallas import tpu as pltpu
from jax.sharding import PartitionSpec as P


HD = 128


epsilon = 1e-05
masked_value = -1e30
key_block = 3584


def _cache_kernel(live_ref, q_ref, k_ref, v_ref, owner_ref, rowreq_ref, m_out, l_out, acc_out, m_s, l_s, acc_s, *, scale):
    i = pl.program_id(0)

    @pl.when(i == 0)
    def _init():
        m_s[...] = jnp.full(m_s.shape, masked_value, jnp.float32)
        l_s[...] = jnp.zeros(l_s.shape, jnp.float32)
        acc_s[...] = jnp.zeros(acc_s.shape, jnp.float32)

    @pl.when(i < live_ref[0])
    def _step():
        scores = lax.dot_general(q_ref[...], k_ref[...], (((1,), (1,)), ((), ())),
                                 preferred_element_type=jnp.float32) * scale
        visible = owner_ref[...] == rowreq_ref[...]
        masked = jnp.where(visible, scores, masked_value)
        running = m_s[...]
        new_max = jnp.maximum(running, jnp.max(masked, axis=1, keepdims=True))
        weights = jnp.where(visible, jnp.exp(masked - new_max), 0.0).astype(jnp.bfloat16)
        factor = jnp.exp(running - new_max)
        l_s[...] = l_s[...] * factor + jnp.sum(weights.astype(jnp.float32), axis=1, keepdims=True)
        acc_s[...] = acc_s[...] * factor + jnp.dot(weights, v_ref[...], preferred_element_type=jnp.float32)
        m_s[...] = new_max

    @pl.when(i == pl.num_programs(0) - 1)
    def _done():
        m_out[...] = m_s[...]
        l_out[...] = l_s[...]
        acc_out[...] = acc_s[...]


def cache_attention(query_rows, cache_keys, cache_values, cache_req, row_req, live_blocks, block, scale):
    rows, hd = query_rows.shape
    pool = cache_keys.shape[0]
    nb = pool // block

    def kv_map(i, live):
        return (jnp.maximum(jnp.minimum(i, live[0] - 1), 0), 0)

    def own_map(i, live):
        return (0, jnp.maximum(jnp.minimum(i, live[0] - 1), 0))

    full = lambda i, live: (0, 0)
    grid_spec = pltpu.PrefetchScalarGridSpec(
        num_scalar_prefetch=1,
        grid=(nb,),
        in_specs=[
            pl.BlockSpec((rows, hd), full),
            pl.BlockSpec((block, hd), kv_map),
            pl.BlockSpec((block, hd), kv_map),
            pl.BlockSpec((1, block), own_map),
            pl.BlockSpec((rows, 1), full),
        ],
        out_specs=[
            pl.BlockSpec((rows, 1), full),
            pl.BlockSpec((rows, 1), full),
            pl.BlockSpec((rows, hd), full),
        ],
        scratch_shapes=[
            pltpu.VMEM((rows, 1), jnp.float32),
            pltpu.VMEM((rows, 1), jnp.float32),
            pltpu.VMEM((rows, hd), jnp.float32),
        ],
    )
    flops = 4 * rows * pool * hd
    cost = pl.CostEstimate(flops=flops, transcendentals=rows * pool,
                           bytes_accessed=2 * pool * hd * 2 + pool * 4 + rows * hd * 6)
    m, l, acc = pl.pallas_call(
        functools.partial(_cache_kernel, scale=scale),
        grid_spec=grid_spec,
        out_shape=[
            jax.ShapeDtypeStruct((rows, 1), jnp.float32),
            jax.ShapeDtypeStruct((rows, 1), jnp.float32),
            jax.ShapeDtypeStruct((rows, hd), jnp.float32),
        ],
        compiler_params=pltpu.CompilerParams(dimension_semantics=("arbitrary",)),
        cost_estimate=cost,
    )(live_blocks.reshape(1).astype(jnp.int32), query_rows, cache_keys, cache_values,
      cache_req.reshape(1, pool), row_req.reshape(rows, 1))
    return m[:, 0], l[:, 0], acc


def attend(queries, new_keys, new_values, cache_keys, cache_values, tok_req, cache_req):
    tokens_here = queries.shape[0]
    head_dim = HD
    kv_here = new_keys.shape[1] // head_dim
    group_size = queries.shape[1] // (kv_here * head_dim)
    score_scale = 1.0 / math.sqrt(head_dim)
    row_count = tokens_here * group_size
    grouped = queries.reshape(tokens_here, kv_here, group_size, head_dim)
    row_req = jnp.repeat(tok_req, group_size)
    row_tok = jnp.repeat(jnp.arange(tokens_here, dtype=jnp.int32), group_size)
    pool_size = cache_keys.shape[0]
    block_width = min(key_block, pool_size)
    live_slots = jnp.sum((cache_req >= 0).astype(jnp.int32))
    live_blocks = (live_slots + block_width - 1) // block_width

    def update(carried, block_keys, block_values, visible):
        running_max, denominator, weighted = carried[0]
        query_rows = grouped[:, 0].reshape(row_count, head_dim)
        scores = (
            jnp.einsum("qd,kd->qk", query_rows, block_keys, preferred_element_type=jnp.float32)
            * score_scale
        )
        masked = jnp.where(visible, scores, masked_value)
        new_max = jnp.maximum(running_max, jnp.max(masked, axis=1))
        weights = jnp.where(visible, jnp.exp(masked - new_max[:, None]), 0.0).astype(jnp.bfloat16)
        factor = jnp.exp(running_max - new_max)
        denominator = denominator * factor + jnp.sum(weights.astype(jnp.float32), axis=1)
        weighted = weighted * factor[:, None] + jnp.dot(
            weights, block_values, preferred_element_type=jnp.float32
        )
        renewed = [(new_max, denominator, weighted)]
        return tuple(renewed)

    initial = tuple(
        (
            (
                jnp.full((row_count,), masked_value, jnp.float32),
                jnp.zeros((row_count,), jnp.float32),
                jnp.zeros((row_count, head_dim), jnp.float32),
            )
            for _ in range(kv_here)
        )
    )

    carried = (
        cache_attention(
            grouped[:, 0].reshape(row_count, head_dim), cache_keys, cache_values,
            cache_req, row_req, live_blocks, block_width, score_scale,
        ),
    )
    causal = (tok_req[None, :] == row_req[:, None]) & (
        jnp.arange(tokens_here, dtype=jnp.int32)[None, :] <= row_tok[:, None]
    )
    carried = update(carried, new_keys, new_values, causal)
    per_head = [
        (weighted / denominator[:, None]).reshape(tokens_here, group_size, head_dim)
        for running_max, denominator, weighted in carried
    ]
    return (
        jnp.stack(per_head, axis=1)
        .reshape(tokens_here, kv_here * group_size * head_dim)
        .astype(jnp.bfloat16)
    )


def per_device(
    queries,
    new_keys,
    new_values,
    cache_keys,
    cache_values,
    tok_req,
    cache_req,
    out_weight,
    residual,
    norm_gain,
    gate_weight,
    up_weight,
    down_weight,
):
    swap = [(0, 1), (1, 0)]
    req_count = lax.axis_size("req")
    y_count = lax.axis_size("y")
    core_count = lax.axis_size("core")
    tokens_out, columns = residual.shape
    gate_partner = lax.ppermute(gate_weight, "core", swap)
    up_partner = lax.ppermute(up_weight, "core", swap)
    down_partner = lax.ppermute(down_weight, "core", swap)
    attended = attend(queries, new_keys, new_values, cache_keys, cache_values, tok_req, cache_req)
    partial_out = jnp.dot(
        lax.all_gather(attended, "req", axis=0, tiled=True),
        out_weight,
        preferred_element_type=jnp.float32,
    )
    core = lax.axis_index("core")
    first_row = (lax.axis_index("y") * core_count + core) * tokens_out
    own_rows = lax.dynamic_slice_in_dim(partial_out, first_row, tokens_out, 0)
    partial_out = lax.dynamic_update_slice_in_dim(
        partial_out, own_rows + residual.astype(jnp.float32), first_row, 0
    )
    parts = partial_out.reshape(y_count, core_count, tokens_out, columns)
    mine = lax.dynamic_index_in_dim(parts, core, 1, keepdims=False)
    theirs = lax.dynamic_index_in_dim(parts, 1 - core, 1, keepdims=False)
    side_partial = mine + lax.ppermute(theirs, "core", swap)
    side_rows = lax.psum(side_partial.astype(jnp.bfloat16), "y")
    stream = lax.dynamic_index_in_dim(side_rows, lax.axis_index("y"), 0, keepdims=False)
    side_rows = side_rows.reshape(y_count * tokens_out, columns)
    side_stream = lax.all_gather(side_rows, "req", axis=1, tiled=True)
    wide_side = side_stream.astype(jnp.float32)
    mean_square = jnp.mean(wide_side * wide_side, axis=1, keepdims=True)
    normed = (wide_side * lax.rsqrt(mean_square + epsilon) * norm_gain[None, :]).astype(
        jnp.bfloat16
    )

    gate_pair = jnp.concatenate([gate_weight, gate_partner], axis=1)
    up_pair = jnp.concatenate([up_weight, up_partner], axis=1)
    down_pair = jnp.concatenate([down_weight, down_partner], axis=0)
    gate = jnp.dot(normed, gate_pair, preferred_element_type=jnp.float32)
    up = jnp.dot(normed, up_pair, preferred_element_type=jnp.float32)
    hidden = (jax.nn.silu(gate) * up).astype(jnp.bfloat16)
    product = jnp.einsum(
        "ysh,hrf->rysf",
        hidden.reshape(y_count, tokens_out, hidden.shape[1]),
        down_pair.reshape(down_pair.shape[0], req_count, columns),
        preferred_element_type=jnp.float32,
    )
    pieces = product.astype(jnp.bfloat16).reshape(req_count * y_count, tokens_out, columns)
    received = lax.all_to_all(pieces, ("req", "y"), 0, 0, tiled=True)
    summed = jnp.sum(received.astype(jnp.float32), axis=0)
    return (stream.astype(jnp.float32) + summed).astype(jnp.bfloat16)


def solution(mesh):
    req_count, tp_count = mesh.devices.shape
    split = jax.sharding.Mesh(
        mesh.devices.reshape(req_count, tp_count // 2, 2), ("req", "y", "core")
    )
    tp = ("y", "core")
    in_specs = (
        P("req", tp),
        P("req", tp),
        P("req", tp),
        P("req", tp),
        P("req", tp),
        P("req"),
        P("req"),
        P(tp, "req"),
        P(tp, "req"),
        P(),
        P(None, ("req",) + tp),
        P(None, ("req",) + tp),
        P(("req",) + tp, None),
    )
    out_specs = P(tp, "req")
    return jax.shard_map(
        per_device, mesh=split, in_specs=in_specs, out_specs=out_specs, check_vma=False
    )
```

```python
import functools
import math

import jax
import jax.numpy as jnp
from jax import lax
from jax.experimental import pallas as pl
from jax.experimental.pallas import tpu as pltpu
from jax.sharding import PartitionSpec as P


HD = 128


epsilon = 1e-05
masked_value = -1e30
key_block = 1792


def _cache_kernel(live_ref, q_ref, k_ref, v_ref, owner_ref, rowreq_ref, nk_ref, nv_ref, tokreq_ref, out_ref, m_s, l_s, acc_s, *, scale, group):
    i = pl.program_id(0)

    @pl.when(i == 0)
    def _init():
        m_s[...] = jnp.full(m_s.shape, masked_value, jnp.float32)
        l_s[...] = jnp.zeros(l_s.shape, jnp.float32)
        acc_s[...] = jnp.zeros(acc_s.shape, jnp.float32)

    @pl.when(i < live_ref[0])
    def _step():
        scores = lax.dot_general(q_ref[...], k_ref[...], (((1,), (1,)), ((), ())),
                                 preferred_element_type=jnp.float32) * scale
        visible = owner_ref[...] == rowreq_ref[...]
        masked = jnp.where(visible, scores, masked_value)
        running = m_s[...]
        new_max = jnp.maximum(running, jnp.max(masked, axis=1, keepdims=True))
        weights = jnp.where(visible, jnp.exp(masked - new_max), 0.0).astype(jnp.bfloat16)
        factor = jnp.exp(running - new_max)
        l_s[...] = l_s[...] * factor + jnp.sum(weights.astype(jnp.float32), axis=1, keepdims=True)
        acc_s[...] = acc_s[...] * factor + jnp.dot(weights, v_ref[...], preferred_element_type=jnp.float32)
        m_s[...] = new_max

    @pl.when(i == pl.num_programs(0) - 1)
    def _done():
        scores = lax.dot_general(q_ref[...], nk_ref[...], (((1,), (1,)), ((), ())),
                                 preferred_element_type=jnp.float32) * scale
        shape = scores.shape
        row_tok = lax.broadcasted_iota(jnp.int32, shape, 0) // group
        col_tok = lax.broadcasted_iota(jnp.int32, shape, 1)
        visible = (tokreq_ref[...] == rowreq_ref[...]) & (col_tok <= row_tok)
        masked = jnp.where(visible, scores, masked_value)
        running = m_s[...]
        new_max = jnp.maximum(running, jnp.max(masked, axis=1, keepdims=True))
        weights = jnp.where(visible, jnp.exp(masked - new_max), 0.0).astype(jnp.bfloat16)
        factor = jnp.exp(running - new_max)
        denominator = l_s[...] * factor + jnp.sum(weights.astype(jnp.float32), axis=1, keepdims=True)
        weighted = acc_s[...] * factor + jnp.dot(weights, nv_ref[...], preferred_element_type=jnp.float32)
        out_ref[...] = (weighted / denominator).astype(out_ref.dtype)


def cache_attention(query_rows, cache_keys, cache_values, cache_req, row_req, live_blocks, block, scale, new_keys, new_values, tok_req, group):
    rows, hd = query_rows.shape
    pool = cache_keys.shape[0]
    nb = pool // block

    def kv_map(i, live):
        return (jnp.maximum(jnp.minimum(i, live[0] - 1), 0), 0)

    def own_map(i, live):
        return (0, jnp.maximum(jnp.minimum(i, live[0] - 1), 0))

    full = lambda i, live: (0, 0)
    grid_spec = pltpu.PrefetchScalarGridSpec(
        num_scalar_prefetch=1,
        grid=(nb,),
        in_specs=[
            pl.BlockSpec((rows, hd), full),
            pl.BlockSpec((block, hd), kv_map),
            pl.BlockSpec((block, hd), kv_map),
            pl.BlockSpec((1, block), own_map),
            pl.BlockSpec((rows, 1), full),
            pl.BlockSpec(new_keys.shape, full),
            pl.BlockSpec(new_values.shape, full),
            pl.BlockSpec((1, tok_req.shape[0]), full),
        ],
        out_specs=pl.BlockSpec((rows, hd), full),
        scratch_shapes=[
            pltpu.VMEM((rows, 1), jnp.float32),
            pltpu.VMEM((rows, 1), jnp.float32),
            pltpu.VMEM((rows, hd), jnp.float32),
        ],
    )
    flops = 4 * rows * pool * hd
    cost = pl.CostEstimate(flops=flops, transcendentals=rows * pool,
                           bytes_accessed=2 * pool * hd * 2 + pool * 4 + rows * hd * 6)
    return pl.pallas_call(
        functools.partial(_cache_kernel, scale=scale, group=group),
        grid_spec=grid_spec,
        out_shape=jax.ShapeDtypeStruct((rows, hd), jnp.bfloat16),
        compiler_params=pltpu.CompilerParams(dimension_semantics=("arbitrary",)),
        cost_estimate=cost,
    )(live_blocks.reshape(1).astype(jnp.int32), query_rows, cache_keys, cache_values,
      cache_req.reshape(1, pool), row_req.reshape(rows, 1), new_keys, new_values,
      tok_req.reshape(1, tok_req.shape[0]))


def attend(queries, new_keys, new_values, cache_keys, cache_values, tok_req, cache_req):
    tokens_here = queries.shape[0]
    head_dim = HD
    kv_here = new_keys.shape[1] // head_dim
    group_size = queries.shape[1] // (kv_here * head_dim)
    score_scale = 1.0 / math.sqrt(head_dim)
    row_count = tokens_here * group_size
    grouped = queries.reshape(tokens_here, kv_here, group_size, head_dim)
    row_req = jnp.repeat(tok_req, group_size)
    row_tok = jnp.repeat(jnp.arange(tokens_here, dtype=jnp.int32), group_size)
    pool_size = cache_keys.shape[0]
    block_width = min(key_block, pool_size)
    live_slots = jnp.sum((cache_req >= 0).astype(jnp.int32))
    live_blocks = (live_slots + block_width - 1) // block_width

    initial = tuple(
        (
            (
                jnp.full((row_count,), masked_value, jnp.float32),
                jnp.zeros((row_count,), jnp.float32),
                jnp.zeros((row_count, head_dim), jnp.float32),
            )
            for _ in range(kv_here)
        )
    )

    result = cache_attention(
        grouped[:, 0].reshape(row_count, head_dim), cache_keys, cache_values,
        cache_req, row_req, live_blocks, block_width, score_scale,
        new_keys, new_values, tok_req, group_size,
    )
    return result.reshape(tokens_here, kv_here * group_size * head_dim)


def per_device(
    queries,
    new_keys,
    new_values,
    cache_keys,
    cache_values,
    tok_req,
    cache_req,
    out_weight,
    residual,
    norm_gain,
    gate_weight,
    up_weight,
    down_weight,
):
    swap = [(0, 1), (1, 0)]
    req_count = lax.axis_size("req")
    y_count = lax.axis_size("y")
    core_count = lax.axis_size("core")
    tokens_out, columns = residual.shape
    gate_partner = lax.ppermute(gate_weight, "core", swap)
    up_partner = lax.ppermute(up_weight, "core", swap)
    down_partner = lax.ppermute(down_weight, "core", swap)
    attended = attend(
        queries, new_keys, new_values, cache_keys, cache_values, tok_req, cache_req
    )
    partial_out = jnp.dot(
        lax.all_gather(attended, "req", axis=0, tiled=True),
        out_weight,
        preferred_element_type=jnp.float32,
    )
    core = lax.axis_index("core")
    first_row = (lax.axis_index("y") * core_count + core) * tokens_out
    own_rows = lax.dynamic_slice_in_dim(partial_out, first_row, tokens_out, 0)
    partial_out = lax.dynamic_update_slice_in_dim(
        partial_out, own_rows + residual.astype(jnp.float32), first_row, 0
    )
    parts = partial_out.reshape(y_count, core_count, tokens_out, columns)
    mine = lax.dynamic_index_in_dim(parts, core, 1, keepdims=False)
    theirs = lax.dynamic_index_in_dim(parts, 1 - core, 1, keepdims=False)
    side_partial = mine + lax.ppermute(theirs, "core", swap)
    side_rows = lax.psum(side_partial, "y").astype(jnp.bfloat16)
    stream = lax.dynamic_index_in_dim(side_rows, lax.axis_index("y"), 0, keepdims=False)
    side_rows = side_rows.reshape(y_count * tokens_out, columns)
    side_stream = lax.all_gather(side_rows, "req", axis=1, tiled=True)
    wide_side = side_stream.astype(jnp.float32)
    mean_square = jnp.mean(wide_side * wide_side, axis=1, keepdims=True)
    normed = (wide_side * lax.rsqrt(mean_square + epsilon) * norm_gain[None, :]).astype(
        jnp.bfloat16
    )

    gate_pair = jnp.concatenate([gate_weight, gate_partner], axis=1)
    up_pair = jnp.concatenate([up_weight, up_partner], axis=1)
    down_pair = jnp.concatenate([down_weight, down_partner], axis=0)
    gate = jnp.dot(normed, gate_pair, preferred_element_type=jnp.float32)
    up = jnp.dot(normed, up_pair, preferred_element_type=jnp.float32)
    hidden = (jax.nn.silu(gate) * up).astype(jnp.bfloat16)
    product = jnp.einsum(
        "ysh,hrf->rysf",
        hidden.reshape(y_count, tokens_out, hidden.shape[1]),
        down_pair.reshape(down_pair.shape[0], req_count, columns),
        preferred_element_type=jnp.float32,
    )
    pieces = product.astype(jnp.bfloat16).reshape(req_count * y_count, tokens_out, columns)
    received = lax.all_to_all(pieces, ("req", "y"), 0, 0, tiled=True)
    summed = jnp.sum(received.astype(jnp.float32), axis=0)
    return (stream.astype(jnp.float32) + summed).astype(jnp.bfloat16)


def solution(mesh):
    req_count, tp_count = mesh.devices.shape
    split = jax.sharding.Mesh(
        mesh.devices.reshape(req_count, tp_count // 2, 2), ("req", "y", "core")
    )
    tp = ("y", "core")
    in_specs = (
        P("req", tp),
        P("req", tp),
        P("req", tp),
        P("req", tp),
        P("req", tp),
        P("req"),
        P("req"),
        P(tp, "req"),
        P(tp, "req"),
        P(),
        P(None, ("req",) + tp),
        P(None, ("req",) + tp),
        P(("req",) + tp, None),
    )
    out_specs = P(tp, "req")
    return jax.shard_map(per_device, mesh=split, in_specs=in_specs, out_specs=out_specs, check_vma=False)
```
